128 devices in a mesh: slab: 32 (over z, y, x_hi), head: 4 (over x_lo, core).
Axes of the slice: x: 4 (x_hi: 2, x_lo: 2; x = x_hi * 2 + x_lo), y: 4, z: 4, core: 2. Of those that a mesh axis runs over, the one named last changes fastest.
Arguments:
- tokens: bfloat16 [65536, 384], P(('slab', 'head')), may hold values from -6 to 6
- norm_gain: float32 [384], replicated, may hold values from 0.25 to 1.75
- w_qkv: bfloat16 [3, 384, 384], replicated, may hold values from -0.3125 to 0.3125
- w_out: bfloat16 [384, 384], replicated, may hold values from -0.625 to 0.625
- cotangent: bfloat16 [65536, 384], P(('slab', 'head')), may hold values from -6 to 6
- neighbours: int32 [512, 8], P('slab'), may hold values from 0 to 511, as said below
- counts: int32 [512], P('slab'), may hold values from 2 to 8, as said below
Outputs:
- output: bfloat16 [65536, 384], P(('slab', 'head'))
- d_tokens: bfloat16 [65536, 384], P(('slab', 'head'))
- d_w_qkv: float32 [3, 384, 384], P(None, None, 'head')
- d_w_out: float32 [384, 384], replicated
- d_gain: float32 [384], replicated
The draws below stay inside these ranges and needn't reach their ends.
Inputs may be any that keep to these rules, and one draw needn't show every extreme that they name: `neighbours`: entry 0 of block b's list is b itself; the entries of a list are distinct and each lies within 16 blocks of b along the periodic block order (modulo 512); every block lists one block at distance exactly 16. Only the first counts[b] slots of block b's list are live; the first block of every slab has all 8 live.
All inputs are finite; a program needn't handle non-finite values.
Results may differ from the reference program's by a relative error of at most 0.024.
Values may be sent and summed in bfloat16 or wider, within the bound.
No kernel may reach another device: no remote copies, remote signals or barrier semaphores. Data moves between devices by JAX's collectives and lax.ppermute only.
A program may use at most 192 MiB of HBM per device.

```python
import math
import jax
import jax.numpy as jnp
from jax import lax

D = 384
HEADS = 12
BLK = 128
NNB = 8
REACH = 16
SLAB_BLK = 16
HD = 32
NBLK = 512
TOKENS = 65536


def draw_neighbours(key, part):
    blocks = jnp.arange(NBLK, dtype=jnp.int32)
    offsets_pool = jnp.concatenate([jnp.arange(1 - REACH, 0, dtype=jnp.int32), jnp.arange(1, REACH, dtype=jnp.int32)])
    pool_size = 2 * REACH - 2
    raw_affinity = jax.random.randint(jax.random.fold_in(key, 11), (NBLK, pool_size), 0, 2 ** 20) * pool_size + jnp.arange(pool_size, dtype=jnp.int32)[None, :]
    ranking = jnp.argsort(raw_affinity, axis=1, stable=True)
    picked = offsets_pool[ranking[:, :NNB - 2]]
    farthest = jnp.where(blocks % 2 == 0, REACH, -REACH).astype(jnp.int32)
    offsets = jnp.concatenate([jnp.zeros((NBLK, 1), jnp.int32), farthest[:, None], picked], 1)
    return ((blocks[:, None] + offsets) % NBLK).astype(jnp.int32)


def draw_counts(key, part):
    n_slabs = NBLK // SLAB_BLK
    density = jax.random.randint(jax.random.fold_in(key, 21), (n_slabs,), 2, NNB + 1)
    jitter = jax.random.randint(jax.random.fold_in(key, 22), (NBLK,), -1, 2)
    counts = jnp.clip(jnp.repeat(density, SLAB_BLK, total_repeat_length=NBLK) + jitter, 2, NNB)
    leading = jnp.arange(NBLK, dtype=jnp.int32) % SLAB_BLK == 0
    return jnp.where(leading, NNB, counts).astype(jnp.int32)


def levels(rng, dims, split, low, largest):
    gain, own = 1.0, jax.random.fold_in(rng, 6)
    for axis_at, parts in split:
        draws = jnp.exp(jax.random.uniform(jax.random.fold_in(own, axis_at), (parts,), jnp.float32, low / len(split), largest / len(split)))
        gain = gain * jnp.repeat(draws, dims[axis_at] // parts).reshape([-1 if axis == axis_at else 1 for axis in range(len(dims))])
    return gain


def centred(own_key, shape, scale, reach, cuts=(), kind=jnp.bfloat16):
    drawn = scale * jax.random.normal(own_key, shape, jnp.float32)
    if cuts:
        drawn = drawn * levels(own_key, shape, cuts, -0.22, 0.18)
    return jnp.clip(drawn, -reach, reach).astype(kind)


def setup_inputs(seed: int = 0) -> dict:
    streams_of = jax.random.split(jax.random.key(seed), 8)
    return {
        "tokens": centred(streams_of[0], (TOKENS, D), 1.0, 6.0, ((0, 128),)),
        "norm_gain": jnp.clip(1.0 + 0.15 * jax.random.normal(streams_of[1], (D,), jnp.float32), 0.25, 1.75),
        "w_qkv": centred(streams_of[2], (3, D, D), D ** -0.5, 0.3125),
        "w_out": centred(streams_of[3], (D, D), (D // 4) ** -0.5, 0.625),
        "cotangent": centred(streams_of[4], (TOKENS, D), 1.0, 6.0, ((0, 128),)),
        "neighbours": draw_neighbours(jax.random.fold_in(streams_of[7], 71), 0),
        "counts": draw_counts(jax.random.fold_in(streams_of[7], 71), 0),
    }


exponent_divisor = 10.0
norm_eps = 1e-06

def normalize(projected, head_dim):
    by_head = projected.reshape(projected.shape[:-1] + (projected.shape[-1] // head_dim, head_dim))
    length = jnp.sqrt(lax.optimization_barrier(jnp.sum(by_head * by_head, -1, keepdims=True)))
    divisor = jnp.maximum(length, 0.7 * math.sqrt(head_dim))
    return (by_head / divisor, divisor, length > 0.7 * math.sqrt(head_dim))

def unit_heads(projected, head_dim):
    unit, divisor, active = normalize(projected, head_dim)
    return unit.reshape(projected.shape)

def norm_back(projected, grad, head_dim):
    unit, divisor, active = normalize(projected, head_dim)
    along = grad.astype(jnp.float32).reshape(unit.shape)
    inner = lax.optimization_barrier(jnp.sum(unit * along, -1, keepdims=True))
    result = (along - jnp.where(active, unit * inner, 0.0)) / divisor
    return result.reshape(projected.shape)

def attention_weights(asking_matrix, lookup_matrix, counts):
    slot_ids = jnp.arange(lookup_matrix.shape[1], dtype=jnp.int32) // asking_matrix.shape[1]
    raw_affinity = exponent_divisor * jnp.einsum('pcxt,pqxt->pxcq', asking_matrix.astype(jnp.float32), lookup_matrix.astype(jnp.float32))
    live_mask = (slot_ids[None, :] < counts[:, None]).astype(jnp.float32)
    raised = jnp.exp(raw_affinity) * live_mask[:, None, None, :]
    return raised / lax.optimization_barrier(jnp.sum(raised, -1, keepdims=True))

def reference(tokens, norm_gain, w_qkv, w_out, cotangent, neighbours, counts):
    tok_f32 = tokens.astype(jnp.float32)
    inverse = lax.rsqrt(lax.optimization_barrier(jnp.mean(tok_f32 * tok_f32, -1, keepdims=True)) + norm_eps)
    normed = (tok_f32 * inverse * norm_gain).astype(jnp.bfloat16)
    projected = jnp.stack([jnp.dot(normed, w_qkv[c], preferred_element_type=jnp.float32) for c in range(3)])
    q_heads = unit_heads(projected[0], HD).astype(jnp.bfloat16)
    k_heads = unit_heads(projected[1], HD).astype(jnp.bfloat16)
    v_heads = projected[2].astype(jnp.bfloat16)
    group_size = 8 if SLAB_BLK % 8 == 0 else SLAB_BLK
    n_groups = NBLK // group_size
    key_blocks = jnp.stack([k_heads, v_heads]).reshape(2, NBLK, BLK, HEADS, HD)
    query_groups = q_heads.reshape(n_groups, group_size, BLK, HEADS, HD)
    lookup_groups = neighbours.reshape(n_groups, group_size, NNB)
    count_groups = counts.reshape(n_groups, group_size)

    def fetch(lookup_rows):
        both = key_blocks[:, lookup_rows.reshape(-1)]
        return both.reshape(2, group_size, NNB * BLK, HEADS, HD)

    def attend(inputs):
        asking_matrix, lookup_rows, live = inputs
        both = fetch(lookup_rows)
        weights_bf = attention_weights(asking_matrix, both[0], live).astype(jnp.bfloat16)
        result = jnp.einsum('ghqk,gkhd->gqhd', weights_bf.astype(jnp.float32), both[1].astype(jnp.float32))
        return result.astype(jnp.bfloat16)
    attended = lax.map(attend, (query_groups, lookup_groups, count_groups)).reshape(TOKENS, D)
    output = (tok_f32 + jnp.dot(attended, w_out, preferred_element_type=jnp.float32)).astype(jnp.bfloat16)
    d_w_out = jnp.dot(attended.T, cotangent, preferred_element_type=jnp.float32)
    d_attended = jnp.dot(cotangent, w_out.T, preferred_element_type=jnp.float32).astype(jnp.bfloat16)
    d_groups = d_attended.reshape(n_groups, group_size, BLK, HEADS, HD)

    def backward_group(grad_buffer, inputs):
        asking_matrix, d_attn, lookup_rows, live = inputs
        both = fetch(lookup_rows)
        normalized_affinity = attention_weights(asking_matrix, both[0], live)
        weights_bf = normalized_affinity.astype(jnp.bfloat16)
        affinity_share_cotangent = jnp.einsum('pcxt,pqxt->pxcq', d_attn.astype(jnp.float32), both[1].astype(jnp.float32))
        pairwise_dot_sum = lax.optimization_barrier(jnp.sum(affinity_share_cotangent * normalized_affinity, -1, keepdims=True))
        affinity_cotangent = (exponent_divisor * normalized_affinity * (affinity_share_cotangent - pairwise_dot_sum)).astype(jnp.bfloat16).astype(jnp.float32)
        d_query = jnp.einsum('ghqk,gkhd->gqhd', affinity_cotangent, both[0].astype(jnp.float32))
        d_keys = jnp.einsum('ghqk,gqhd->gkhd', affinity_cotangent, asking_matrix.astype(jnp.float32))
        d_values = jnp.einsum('ghqk,gqhd->gkhd', weights_bf.astype(jnp.float32), d_attn.astype(jnp.float32))
        stacked = jnp.stack([d_keys, d_values]).reshape(2, group_size * NNB, BLK, HEADS, HD)
        grad_buffer = grad_buffer.at[:, lookup_rows.reshape(-1)].add(stacked)
        return (grad_buffer, d_query)
    start_buffer = jnp.zeros((2, NBLK, BLK, HEADS, HD), jnp.float32)
    grad_buffer, d_query_groups = lax.scan(backward_group, start_buffer, (query_groups, d_groups, lookup_groups, count_groups))
    dq_heads = d_query_groups.reshape(TOKENS, D).astype(jnp.bfloat16)
    dk_heads = grad_buffer[0].reshape(TOKENS, D).astype(jnp.bfloat16)
    dv_heads = grad_buffer[1].reshape(TOKENS, D).astype(jnp.bfloat16)
    d_q = norm_back(projected[0], dq_heads, HD).astype(jnp.bfloat16)
    d_k = norm_back(projected[1], dk_heads, HD).astype(jnp.bfloat16)
    d_qkv = [d_q, d_k, dv_heads]
    d_normed = jnp.dot(d_qkv[0], w_qkv[0].T, preferred_element_type=jnp.float32)
    d_normed = d_normed + jnp.dot(d_qkv[1], w_qkv[1].T, preferred_element_type=jnp.float32)
    d_normed = d_normed + jnp.dot(d_qkv[2], w_qkv[2].T, preferred_element_type=jnp.float32)
    d_w_qkv = jnp.stack([jnp.dot(normed.T, d_qkv[c], preferred_element_type=jnp.float32) for c in range(3)])
    d_gain = lax.optimization_barrier(jnp.sum(d_normed * tok_f32 * inverse, 0))
    scaled = d_normed * norm_gain
    d_tokens = cotangent.astype(jnp.float32) + inverse * scaled - tok_f32 * inverse ** 3 * lax.optimization_barrier(jnp.mean(scaled * tok_f32, -1, keepdims=True))
    return (output, d_tokens.astype(jnp.bfloat16), d_w_qkv, d_w_out, d_gain)
```

```python
import math

import jax
import jax.numpy as jnp
from jax import lax
from jax.sharding import PartitionSpec as P

HEADS = 12
BLK = 128
REACH = 16


exponent_divisor = 10.0
norm_eps = 1e-06


def padded(value, sides, width):
    for axis, dim in sides:
        size, length = (lax.axis_size(axis), value.shape[dim])
        up = [(i, (i + 1) % size) for i in range(size)]
        down = [(j, i) for i, j in up]
        last = lax.slice_in_dim(value, length - width, length, axis=dim)
        first = lax.slice_in_dim(value, 0, width, axis=dim)
        before = lax.ppermute(last, axis, up)
        after = lax.ppermute(first, axis, down)
        value = jnp.concatenate([before, value, after], axis=dim)
    return value


def passed_along(value, axis, steps):
    count = lax.axis_size(axis)
    pairs = [(source, (source + steps) % count) for source in range(count)]
    return lax.ppermute(value, axis, pairs)


def normalize(projected, head_dim):
    by_head = projected.reshape(projected.shape[:-1] + (projected.shape[-1] // head_dim, head_dim))
    length = jnp.sqrt(jnp.sum(by_head * by_head, -1, keepdims=True))
    divisor = jnp.maximum(length, 0.7 * math.sqrt(head_dim))
    return (by_head / divisor, divisor, length > 0.7 * math.sqrt(head_dim))


def unit_heads(projected, head_dim):
    unit, divisor, active = normalize(projected, head_dim)
    return unit.reshape(projected.shape)


def norm_back(projected, grad, head_dim):
    unit, divisor, active = normalize(projected, head_dim)
    along = grad.astype(jnp.float32).reshape(unit.shape)
    inner = jnp.sum(unit * along, -1, keepdims=True)
    result = (along - jnp.where(active, unit * inner, 0.0)) / divisor
    return result.reshape(projected.shape)


def to_heads(value, blocks, heads_here, head_dim):
    lead = value.shape[:-2]
    value = value.reshape(lead + (blocks, BLK, heads_here, head_dim))
    return jnp.moveaxis(value, len(lead) + 2, len(lead))


def from_heads(value):
    lead = value.shape[:-4]
    heads_here, blocks, rows, head_dim = value.shape[len(lead) :]
    value = jnp.moveaxis(value, len(lead), len(lead) + 2)
    return value.reshape(lead + (blocks * rows, heads_here * head_dim))


def local(tokens, norm_gain, w_qkv, w_out, cotangent, neighbours, counts):
    f32, bf16 = jnp.float32, jnp.bfloat16
    width = tokens.shape[1]
    head_dim = width // HEADS
    n_head = lax.axis_size("head")
    n_slab = lax.axis_size("slab")
    head_cols = width // n_head
    heads_here = HEADS // n_head
    head_index = lax.axis_index("head")
    slab_index = lax.axis_index("slab")
    slab_blocks, n_slots = neighbours.shape
    ext_blocks = slab_blocks + 2 * REACH
    n_blocks = slab_blocks * n_slab
    tok_f32 = tokens.astype(f32)
    inverse = lax.rsqrt(jnp.mean(tok_f32 * tok_f32, -1, keepdims=True) + norm_eps)
    normed = (tok_f32 * inverse * norm_gain).astype(bf16)
    w_here = lax.dynamic_slice_in_dim(w_qkv, head_index * head_cols, head_cols, 2)
    gathered = lax.all_gather(normed, "head", axis=0, tiled=True)
    projected = jnp.einsum("rd,cde->cre", gathered, w_here, preferred_element_type=f32)
    packed = jnp.stack(
        [unit_heads(projected[0], head_dim), unit_heads(projected[1], head_dim), projected[2]]
    ).astype(bf16)
    split = lambda value: to_heads(value, slab_blocks, heads_here, head_dim)
    q_heads = split(packed[0])
    keys_values = split(packed[1:])
    extended = padded(keys_values, (("slab", 2),), REACH)
    lookup = (neighbours - slab_index * slab_blocks + REACH) % n_blocks
    choose = lookup[:, :, None] == jnp.arange(ext_blocks, dtype=jnp.int32)
    fetched = jnp.einsum(
        "bse,chekd->chbskd", choose.astype(bf16), extended, preferred_element_type=f32
    ).astype(bf16)
    keys, values = fetched[0], fetched[1]
    live = (jnp.arange(n_slots, dtype=jnp.int32)[None, :] < counts[:, None]).astype(f32)
    scores = exponent_divisor * jnp.einsum(
        "hbqd,hbskd->hbqsk", q_heads, keys, preferred_element_type=f32
    )
    raised = jnp.exp(scores) * live[None, :, None, :, None]
    weights = raised / jnp.sum(raised, (-2, -1), keepdims=True)
    weights_bf = weights.astype(bf16)
    attended_heads = jnp.einsum(
        "hbqsk,hbskd->hbqd", weights_bf, values, preferred_element_type=f32
    ).astype(bf16)
    attended = lax.all_to_all(
        from_heads(attended_heads), "head", split_axis=0, concat_axis=1, tiled=True
    )
    output = (tok_f32 + jnp.dot(attended, w_out, preferred_element_type=f32)).astype(bf16)
    d_out_part = jnp.dot(attended.T, cotangent, preferred_element_type=f32)
    d_attended = jnp.dot(cotangent, w_out.T, preferred_element_type=f32).astype(bf16)
    d_attn = split(lax.all_to_all(d_attended, "head", split_axis=1, concat_axis=0, tiled=True))
    d_weights = jnp.einsum("hbqd,hbskd->hbqsk", d_attn, values, preferred_element_type=f32)
    row_dot = jnp.sum(d_weights * weights, (-2, -1), keepdims=True)
    d_scores = (exponent_divisor * weights * (d_weights - row_dot)).astype(bf16)
    d_query = jnp.einsum("hbqsk,hbskd->hbqd", d_scores, keys, preferred_element_type=f32)
    d_keys = jnp.einsum("hbqsk,hbqd->hbskd", d_scores, q_heads, preferred_element_type=f32)
    d_values = jnp.einsum("hbqsk,hbqd->hbskd", weights_bf, d_attn, preferred_element_type=f32)
    grad_ext = jnp.einsum(
        "bse,chbskd->chekd",
        choose.astype(f32),
        jnp.stack([d_keys, d_values]),
        precision=lax.Precision.HIGHEST,
        preferred_element_type=f32,
    )
    low_rim = grad_ext[:, :, :REACH]
    high_rim = grad_ext[:, :, REACH + slab_blocks :]
    from_above = passed_along(low_rim.astype(bf16), "slab", -1).astype(f32)
    from_below = passed_along(high_rim, "slab", 1)
    own_grads = grad_ext[:, :, REACH : REACH + slab_blocks]
    own_grads = own_grads.at[:, :, slab_blocks - REACH :].add(from_above)
    own_grads = own_grads.at[:, :, :REACH].add(from_below)
    d_packed = jnp.concatenate(
        [from_heads(d_query)[None], from_heads(own_grads)], 0
    ).astype(bf16)
    d_query_part = norm_back(projected[0], d_packed[0], head_dim).astype(bf16)
    d_key_part = norm_back(projected[1], d_packed[1], head_dim).astype(bf16)
    d_qkv = jnp.stack([d_query_part, d_key_part, d_packed[2]])
    d_normed = lax.psum_scatter(
        jnp.einsum("crk,cdk->rd", d_qkv, w_here, preferred_element_type=f32).astype(bf16),
        "head",
        scatter_dimension=0,
        tiled=True,
    ).astype(f32)
    d_qkv_part = jnp.einsum("rd,crk->cdk", gathered, d_qkv, preferred_element_type=f32)
    d_gain_part = jnp.sum(d_normed * tok_f32 * inverse, 0)
    slots = jnp.zeros((n_head,) + d_qkv_part.shape, f32)
    slots = lax.dynamic_update_index_in_dim(slots, d_qkv_part, head_index, 0)
    pieces = [slots.reshape(-1, width), d_out_part, d_gain_part[None]]
    total = lax.psum(jnp.concatenate(pieces, 0), ("slab", "head"))
    slot_rows = pieces[0].shape[0]
    all_slots = total[:slot_rows].reshape(slots.shape)
    d_w_qkv = lax.dynamic_index_in_dim(all_slots, head_index, 0, keepdims=False)
    d_w_out = total[slot_rows : slot_rows + width]
    d_gain = total[slot_rows + width]
    scaled = d_normed * norm_gain
    d_tokens = (
        cotangent.astype(f32)
        + inverse * scaled
        - tok_f32 * inverse**3 * jnp.mean(scaled * tok_f32, -1, keepdims=True)
    )
    return (output, d_tokens.astype(bf16), d_w_qkv, d_w_out, d_gain)


def solution(mesh):
    placed = (
        P(("slab", "head"), None),
        P(),
        P(),
        P(),
        P(("slab", "head"), None),
        P("slab", None),
        P("slab"),
    )
    return jax.shard_map(
        local,
        mesh=mesh,
        in_specs=placed,
        out_specs=(
            P(("slab", "head"), None),
            P(("slab", "head"), None),
            P(None, None, "head"),
            P(),
            P(),
        ),
        check_vma=False,
    )
```

```python
import math

import jax
import jax.numpy as jnp
from jax import lax
from jax.sharding import PartitionSpec as P

HEADS = 12
BLK = 128
REACH = 16


exponent_divisor = 10.0
norm_eps = 1e-06


def padded(value, sides, width):
    for axis, dim in sides:
        size, length = (lax.axis_size(axis), value.shape[dim])
        up = [(i, (i + 1) % size) for i in range(size)]
        down = [(j, i) for i, j in up]
        last = lax.slice_in_dim(value, length - width, length, axis=dim)
        first = lax.slice_in_dim(value, 0, width, axis=dim)
        before = lax.ppermute(last, axis, up)
        after = lax.ppermute(first, axis, down)
        value = jnp.concatenate([before, value, after], axis=dim)
    return value


def passed_along(value, axis, steps):
    count = lax.axis_size(axis)
    pairs = [(source, (source + steps) % count) for source in range(count)]
    return lax.ppermute(value, axis, pairs)


def normalize(projected, head_dim):
    by_head = projected.reshape(projected.shape[:-1] + (projected.shape[-1] // head_dim, head_dim))
    length = jnp.sqrt(jnp.sum(by_head * by_head, -1, keepdims=True))
    divisor = jnp.maximum(length, 0.7 * math.sqrt(head_dim))
    return (by_head / divisor, divisor, length > 0.7 * math.sqrt(head_dim))


def unit_heads(projected, head_dim):
    unit, divisor, active = normalize(projected, head_dim)
    return unit.reshape(projected.shape)


def norm_back(projected, grad, head_dim):
    unit, divisor, active = normalize(projected, head_dim)
    along = grad.astype(jnp.float32).reshape(unit.shape)
    inner = jnp.sum(unit * along, -1, keepdims=True)
    result = (along - jnp.where(active, unit * inner, 0.0)) / divisor
    return result.reshape(projected.shape)


def to_heads(value, blocks, heads_here, head_dim):
    lead = value.shape[:-2]
    value = value.reshape(lead + (blocks, BLK, heads_here, head_dim))
    return jnp.moveaxis(value, len(lead) + 2, len(lead))


def from_heads(value):
    lead = value.shape[:-4]
    heads_here, blocks, rows, head_dim = value.shape[len(lead) :]
    value = jnp.moveaxis(value, len(lead), len(lead) + 2)
    return value.reshape(lead + (blocks * rows, heads_here * head_dim))


def local(tokens, norm_gain, w_qkv, w_out, cotangent, neighbours, counts):
    f32, bf16 = jnp.float32, jnp.bfloat16
    width = tokens.shape[1]
    head_dim = width // HEADS
    n_head = lax.axis_size("head")
    n_slab = lax.axis_size("slab")
    head_cols = width // n_head
    heads_here = HEADS // n_head
    head_index = lax.axis_index("head")
    slab_index = lax.axis_index("slab")
    slab_blocks, n_slots = neighbours.shape
    ext_blocks = slab_blocks + 2 * REACH
    n_blocks = slab_blocks * n_slab
    tok_f32 = tokens.astype(f32)
    inverse = lax.rsqrt(jnp.mean(tok_f32 * tok_f32, -1, keepdims=True) + norm_eps)
    normed = (tok_f32 * inverse * norm_gain).astype(bf16)
    w_here = lax.dynamic_slice_in_dim(w_qkv, head_index * head_cols, head_cols, 2)
    gathered = lax.all_gather(normed, "head", axis=0, tiled=True)
    projected = jnp.einsum("rd,cde->cre", gathered, w_here, preferred_element_type=f32)
    packed = jnp.stack(
        [unit_heads(projected[0], head_dim), unit_heads(projected[1], head_dim), projected[2]]
    ).astype(bf16)
    split = lambda value: to_heads(value, slab_blocks, heads_here, head_dim)
    q_heads = split(packed[0])
    keys_values = split(packed[1:])
    extended = padded(keys_values, (("slab", 2),), REACH)
    lookup = (neighbours - slab_index * slab_blocks + REACH) % n_blocks
    choose = lookup[:, :, None] == jnp.arange(ext_blocks, dtype=jnp.int32)
    fetched = jnp.einsum(
        "bse,chekd->chbskd", choose.astype(bf16), extended, preferred_element_type=f32
    ).astype(bf16)
    keys, values = fetched[0], fetched[1]
    live = (jnp.arange(n_slots, dtype=jnp.int32)[None, :] < counts[:, None]).astype(f32)
    scores = exponent_divisor * jnp.einsum(
        "hbqd,hbskd->hbqsk", q_heads, keys, preferred_element_type=f32
    )
    raised = jnp.exp(scores) * live[None, :, None, :, None]
    weights = raised / jnp.sum(raised, (-2, -1), keepdims=True)
    weights_bf = weights.astype(bf16)
    attended_heads = jnp.einsum(
        "hbqsk,hbskd->hbqd", weights_bf, values, preferred_element_type=f32
    ).astype(bf16)
    attended = lax.all_to_all(
        from_heads(attended_heads), "head", split_axis=0, concat_axis=1, tiled=True
    )
    output = (tok_f32 + jnp.dot(attended, w_out, preferred_element_type=f32)).astype(bf16)
    d_out_part = jnp.dot(attended.T, cotangent, preferred_element_type=f32)
    d_attended = jnp.dot(cotangent, w_out.T, preferred_element_type=f32).astype(bf16)
    d_attn = split(lax.all_to_all(d_attended, "head", split_axis=1, concat_axis=0, tiled=True))
    d_weights = jnp.einsum("hbqd,hbskd->hbqsk", d_attn, values, preferred_element_type=f32)
    row_dot = jnp.sum(d_weights * weights, (-2, -1), keepdims=True)
    d_scores = (exponent_divisor * weights * (d_weights - row_dot)).astype(bf16)
    d_query = jnp.einsum("hbqsk,hbskd->hbqd", d_scores, keys, preferred_element_type=f32)
    d_keys = jnp.einsum("hbqsk,hbqd->hbskd", d_scores, q_heads, preferred_element_type=f32)
    d_values = jnp.einsum("hbqsk,hbqd->hbskd", weights_bf, d_attn, preferred_element_type=f32)
    scatter = lambda grads: jnp.einsum(
        "bse,hbskd->hekd",
        choose.astype(f32),
        grads,
        precision=lax.Precision.HIGHEST,
        preferred_element_type=f32,
    )
    grad_ext = jnp.stack([scatter(d_keys), scatter(d_values)])
    low_rim = grad_ext[:, :, :REACH]
    high_rim = grad_ext[:, :, REACH + slab_blocks :]
    from_above = passed_along(low_rim.astype(bf16), "slab", -1).astype(f32)
    from_below = passed_along(high_rim.astype(bf16), "slab", 1).astype(f32)
    own_grads = grad_ext[:, :, REACH : REACH + slab_blocks]
    own_grads = own_grads.at[:, :, slab_blocks - REACH :].add(from_above)
    own_grads = own_grads.at[:, :, :REACH].add(from_below)
    d_packed = jnp.concatenate(
        [from_heads(d_query)[None], from_heads(own_grads)], 0
    ).astype(bf16)
    d_query_part = norm_back(projected[0], d_packed[0], head_dim).astype(bf16)
    d_key_part = norm_back(projected[1], d_packed[1], head_dim).astype(bf16)
    d_qkv = jnp.stack([d_query_part, d_key_part, d_packed[2]])
    d_normed = lax.psum_scatter(
        jnp.einsum("crk,cdk->rd", d_qkv, w_here, preferred_element_type=f32).astype(bf16),
        "head",
        scatter_dimension=0,
        tiled=True,
    ).astype(f32)
    d_qkv_part = jnp.einsum("rd,crk->cdk", gathered, d_qkv, preferred_element_type=f32)
    d_gain_part = jnp.sum(d_normed * tok_f32 * inverse, 0)
    slots = jnp.zeros((n_head,) + d_qkv_part.shape, f32)
    slots = lax.dynamic_update_index_in_dim(slots, d_qkv_part, head_index, 0)
    pieces = [slots.reshape(-1, width), d_out_part, d_gain_part[None]]
    total = lax.psum(jnp.concatenate(pieces, 0), ("slab", "head"))
    slot_rows = pieces[0].shape[0]
    all_slots = total[:slot_rows].reshape(slots.shape)
    d_w_qkv = lax.dynamic_index_in_dim(all_slots, head_index, 0, keepdims=False)
    d_w_out = total[slot_rows : slot_rows + width]
    d_gain = total[slot_rows + width]
    scaled = d_normed * norm_gain
    d_tokens = (
        cotangent.astype(f32)
        + inverse * scaled
        - tok_f32 * inverse**3 * jnp.mean(scaled * tok_f32, -1, keepdims=True)
    )
    return (output, d_tokens.astype(bf16), d_w_qkv, d_w_out, d_gain)


def solution(mesh):
    placed = (
        P(("slab", "head"), None),
        P(),
        P(),
        P(),
        P(("slab", "head"), None),
        P("slab", None),
        P("slab"),
    )
    return jax.shard_map(
        local,
        mesh=mesh,
        in_specs=placed,
        out_specs=(
            P(("slab", "head"), None),
            P(("slab", "head"), None),
            P(None, None, "head"),
            P(),
            P(),
        ),
        check_vma=False,
    )
```

```python
import math

import jax
import jax.numpy as jnp
from jax import lax
from jax.sharding import PartitionSpec as P

HEADS = 12
BLK = 128
REACH = 16


exponent_divisor = 10.0
norm_eps = 1e-06


def padded(value, sides, width):
    for axis, dim in sides:
        size, length = (lax.axis_size(axis), value.shape[dim])
        up = [(i, (i + 1) % size) for i in range(size)]
        down = [(j, i) for i, j in up]
        last = lax.slice_in_dim(value, length - width, length, axis=dim)
        first = lax.slice_in_dim(value, 0, width, axis=dim)
        before = lax.ppermute(last, axis, up)
        after = lax.ppermute(first, axis, down)
        value = jnp.concatenate([before, value, after], axis=dim)
    return value


def passed_along(value, axis, steps):
    count = lax.axis_size(axis)
    pairs = [(source, (source + steps) % count) for source in range(count)]
    return lax.ppermute(value, axis, pairs)


def normalize(projected, head_dim):
    by_head = projected.reshape(projected.shape[:-1] + (projected.shape[-1] // head_dim, head_dim))
    length = jnp.sqrt(jnp.sum(by_head * by_head, -1, keepdims=True))
    divisor = jnp.maximum(length, 0.7 * math.sqrt(head_dim))
    return (by_head / divisor, divisor, length > 0.7 * math.sqrt(head_dim))


def unit_heads(projected, head_dim):
    unit, divisor, active = normalize(projected, head_dim)
    return unit.reshape(projected.shape)


def norm_back(projected, grad, head_dim):
    unit, divisor, active = normalize(projected, head_dim)
    along = grad.astype(jnp.float32).reshape(unit.shape)
    inner = jnp.sum(unit * along, -1, keepdims=True)
    result = (along - jnp.where(active, unit * inner, 0.0)) / divisor
    return result.reshape(projected.shape)


def to_heads(value, blocks, heads_here, head_dim):
    lead = value.shape[:-2]
    value = value.reshape(lead + (blocks, BLK, heads_here, head_dim))
    return jnp.moveaxis(value, len(lead) + 2, len(lead))


def from_heads(value):
    lead = value.shape[:-4]
    heads_here, blocks, rows, head_dim = value.shape[len(lead) :]
    value = jnp.moveaxis(value, len(lead), len(lead) + 2)
    return value.reshape(lead + (blocks * rows, heads_here * head_dim))


def local(tokens, norm_gain, w_qkv, w_out, cotangent, neighbours, counts):
    f32, bf16 = jnp.float32, jnp.bfloat16
    width = tokens.shape[1]
    head_dim = width // HEADS
    n_head = lax.axis_size("head")
    n_slab = lax.axis_size("slab")
    head_cols = width // n_head
    heads_here = HEADS // n_head
    head_index = lax.axis_index("head")
    slab_index = lax.axis_index("slab")
    slab_blocks, n_slots = neighbours.shape
    ext_blocks = slab_blocks + 2 * REACH
    n_blocks = slab_blocks * n_slab
    tok_f32 = tokens.astype(f32)
    inverse = lax.rsqrt(jnp.mean(tok_f32 * tok_f32, -1, keepdims=True) + norm_eps)
    normed = (tok_f32 * inverse * norm_gain).astype(bf16)
    w_here = lax.dynamic_slice_in_dim(w_qkv, head_index * head_cols, head_cols, 2)
    slab_tok = lax.all_gather(tokens, "head", axis=0, tiled=True).astype(f32)
    slab_inverse = lax.rsqrt(jnp.mean(slab_tok * slab_tok, -1, keepdims=True) + norm_eps)
    slab_scaled = slab_tok * slab_inverse
    gathered = (slab_scaled * norm_gain).astype(bf16)
    projected = jnp.einsum("rd,cde->cre", gathered, w_here, preferred_element_type=f32)
    packed = jnp.stack(
        [unit_heads(projected[0], head_dim), unit_heads(projected[1], head_dim), projected[2]]
    ).astype(bf16)
    split = lambda value: to_heads(value, slab_blocks, heads_here, head_dim)
    q_heads = split(packed[0])
    keys_values = split(packed[1:])
    extended = padded(keys_values, (("slab", 2),), REACH)
    lookup = (neighbours - slab_index * slab_blocks + REACH) % n_blocks
    choose = lookup[:, :, None] == jnp.arange(ext_blocks, dtype=jnp.int32)
    fetched = jnp.einsum(
        "bse,chekd->chbskd", choose.astype(bf16), extended, preferred_element_type=f32
    ).astype(bf16)
    keys, values = fetched[0], fetched[1]
    live = (jnp.arange(n_slots, dtype=jnp.int32)[None, :] < counts[:, None]).astype(f32)
    scores = exponent_divisor * jnp.einsum(
        "hbqd,hbskd->hbqsk", q_heads, keys, preferred_element_type=f32
    )
    raised = jnp.exp(scores) * live[None, :, None, :, None]
    weights = raised / jnp.sum(raised, (-2, -1), keepdims=True)
    weights_bf = weights.astype(bf16)
    attended_heads = jnp.einsum(
        "hbqsk,hbskd->hbqd", weights_bf, values, preferred_element_type=f32
    ).astype(bf16)
    attended = lax.all_to_all(
        from_heads(attended_heads), "head", split_axis=0, concat_axis=1, tiled=True
    )
    output = (tok_f32 + jnp.dot(attended, w_out, preferred_element_type=f32)).astype(bf16)
    d_out_part = jnp.dot(attended.T, cotangent, preferred_element_type=f32)
    d_attended = jnp.dot(cotangent, w_out.T, preferred_element_type=f32).astype(bf16)
    d_attn = split(lax.all_to_all(d_attended, "head", split_axis=1, concat_axis=0, tiled=True))
    d_weights = jnp.einsum("hbqd,hbskd->hbqsk", d_attn, values, preferred_element_type=f32)
    row_dot = jnp.sum(d_weights * weights, (-2, -1), keepdims=True)
    d_scores = (exponent_divisor * weights * (d_weights - row_dot)).astype(bf16)
    d_query = jnp.einsum("hbqsk,hbskd->hbqd", d_scores, keys, preferred_element_type=f32)
    d_keys = jnp.einsum("hbqsk,hbqd->hbskd", d_scores, q_heads, preferred_element_type=f32)
    d_values = jnp.einsum("hbqsk,hbqd->hbskd", weights_bf, d_attn, preferred_element_type=f32)
    scatter = lambda grads: jnp.einsum(
        "bse,hbskd->hekd",
        choose.astype(f32),
        grads,
        precision=lax.Precision.HIGHEST,
        preferred_element_type=f32,
    )
    grad_ext = jnp.stack([scatter(d_keys), scatter(d_values)])
    low_rim = grad_ext[:, :, :REACH]
    high_rim = grad_ext[:, :, REACH + slab_blocks :]
    from_above = passed_along(low_rim.astype(bf16), "slab", -1).astype(f32)
    from_below = passed_along(high_rim.astype(bf16), "slab", 1).astype(f32)
    own_grads = grad_ext[:, :, REACH : REACH + slab_blocks]
    own_grads = own_grads.at[:, :, slab_blocks - REACH :].add(from_above)
    own_grads = own_grads.at[:, :, :REACH].add(from_below)
    d_packed = jnp.concatenate(
        [from_heads(d_query)[None], from_heads(own_grads)], 0
    ).astype(bf16)
    d_query_part = norm_back(projected[0], d_packed[0], head_dim).astype(bf16)
    d_key_part = norm_back(projected[1], d_packed[1], head_dim).astype(bf16)
    d_qkv = jnp.stack([d_query_part, d_key_part, d_packed[2]])
    d_normed_part = jnp.einsum("crk,cdk->rd", d_qkv, w_here, preferred_element_type=f32)
    d_gain_part = jnp.sum(d_normed_part * slab_scaled, 0)
    shares = d_normed_part.astype(bf16).reshape(n_head, -1, width)
    d_normed = jnp.sum(
        lax.all_to_all(shares, "head", split_axis=0, concat_axis=0, tiled=True).astype(f32), 0
    )
    d_qkv_part = jnp.einsum("rd,crk->cdk", gathered, d_qkv, preferred_element_type=f32)
    slots = jnp.zeros((n_head,) + d_qkv_part.shape, f32)
    slots = lax.dynamic_update_index_in_dim(slots, d_qkv_part, head_index, 0)
    pieces = [slots.reshape(-1, width), d_out_part, d_gain_part[None]]
    total = lax.psum(jnp.concatenate(pieces, 0), ("slab", "head"))
    slot_rows = pieces[0].shape[0]
    all_slots = total[:slot_rows].reshape(slots.shape)
    d_w_qkv = lax.dynamic_index_in_dim(all_slots, head_index, 0, keepdims=False)
    d_w_out = total[slot_rows : slot_rows + width]
    d_gain = total[slot_rows + width]
    scaled = d_normed * norm_gain
    d_tokens = (
        cotangent.astype(f32)
        + inverse * scaled
        - tok_f32 * inverse**3 * jnp.mean(scaled * tok_f32, -1, keepdims=True)
    )
    return (output, d_tokens.astype(bf16), d_w_qkv, d_w_out, d_gain)


def solution(mesh):
    placed = (
        P(("slab", "head"), None),
        P(),
        P(),
        P(),
        P(("slab", "head"), None),
        P("slab", None),
        P("slab"),
    )
    return jax.shard_map(
        local,
        mesh=mesh,
        in_specs=placed,
        out_specs=(
            P(("slab", "head"), None),
            P(("slab", "head"), None),
            P(None, None, "head"),
            P(),
            P(),
        ),
        check_vma=False,
    )
```

```python
import math

import jax
import jax.numpy as jnp
from jax import lax
from jax.sharding import PartitionSpec as P

HEADS = 12
BLK = 128
REACH = 16


exponent_divisor = 10.0
norm_eps = 1e-06


def padded(value, sides, width):
    for axis, dim in sides:
        size, length = (lax.axis_size(axis), value.shape[dim])
        up = [(i, (i + 1) % size) for i in range(size)]
        down = [(j, i) for i, j in up]
        last = lax.slice_in_dim(value, length - width, length, axis=dim)
        first = lax.slice_in_dim(value, 0, width, axis=dim)
        before = lax.ppermute(last, axis, up)
        after = lax.ppermute(first, axis, down)
        value = jnp.concatenate([before, value, after], axis=dim)
    return value


def passed_along(value, axis, steps):
    count = lax.axis_size(axis)
    pairs = [(source, (source + steps) % count) for source in range(count)]
    return lax.ppermute(value, axis, pairs)


def normalize(projected, head_dim):
    by_head = projected.reshape(projected.shape[:-1] + (projected.shape[-1] // head_dim, head_dim))
    length = jnp.sqrt(jnp.sum(by_head * by_head, -1, keepdims=True))
    divisor = jnp.maximum(length, 0.7 * math.sqrt(head_dim))
    return (by_head / divisor, divisor, length > 0.7 * math.sqrt(head_dim))


def unit_heads(projected, head_dim):
    unit, divisor, active = normalize(projected, head_dim)
    return unit.reshape(projected.shape)


def norm_back(projected, grad, head_dim):
    unit, divisor, active = normalize(projected, head_dim)
    along = grad.astype(jnp.float32).reshape(unit.shape)
    inner = jnp.sum(unit * along, -1, keepdims=True)
    result = (along - jnp.where(active, unit * inner, 0.0)) / divisor
    return result.reshape(projected.shape)


def xor_steps():
    steps = []
    for axis in ("head", "slab"):
        size = lax.axis_size(axis)
        assert size & (size - 1) == 0
        mask = 1
        while mask < size:
            steps.append((axis, mask))
            mask *= 2
    return steps


def xor_swap(value, axis, mask):
    size = lax.axis_size(axis)
    return lax.ppermute(value, axis, [(i, i ^ mask) for i in range(size)])


def ordered_pair(held, received, bit):
    pair = jnp.stack([held, received])
    first = lax.dynamic_index_in_dim(pair, bit, 0, keepdims=False)
    second = lax.dynamic_index_in_dim(pair, 1 - bit, 0, keepdims=False)
    return jnp.concatenate([first, second], 0)


def butterfly_gather(value, axis):
    size = lax.axis_size(axis)
    held = value
    mask = 1
    while mask < size:
        bit = (lax.axis_index(axis) // mask) % 2
        held = ordered_pair(held, xor_swap(held, axis, mask), bit)
        mask *= 2
    return held


def butterfly_psum(value):
    steps = xor_steps()
    held = value
    bits = []
    for axis, mask in steps:
        bit = (lax.axis_index(axis) // mask) % 2
        halves = held.reshape((2, held.shape[0] // 2) + held.shape[1:])
        keep = lax.dynamic_index_in_dim(halves, bit, 0, keepdims=False)
        send = lax.dynamic_index_in_dim(halves, 1 - bit, 0, keepdims=False)
        held = keep + xor_swap(send, axis, mask)
        bits.append(bit)
    for (axis, mask), bit in reversed(list(zip(steps, bits))):
        held = ordered_pair(held, xor_swap(held, axis, mask), bit)
    return held


def to_heads(value, blocks, heads_here, head_dim):
    lead = value.shape[:-2]
    value = value.reshape(lead + (blocks, BLK, heads_here, head_dim))
    return jnp.moveaxis(value, len(lead) + 2, len(lead))


def from_heads(value):
    lead = value.shape[:-4]
    heads_here, blocks, rows, head_dim = value.shape[len(lead) :]
    value = jnp.moveaxis(value, len(lead), len(lead) + 2)
    return value.reshape(lead + (blocks * rows, heads_here * head_dim))


def local(tokens, norm_gain, w_qkv, w_out, cotangent, neighbours, counts):
    f32, bf16 = jnp.float32, jnp.bfloat16
    width = tokens.shape[1]
    head_dim = width // HEADS
    n_head = lax.axis_size("head")
    n_slab = lax.axis_size("slab")
    head_cols = width // n_head
    heads_here = HEADS // n_head
    head_index = lax.axis_index("head")
    slab_index = lax.axis_index("slab")
    slab_blocks, n_slots = neighbours.shape
    ext_blocks = slab_blocks + 2 * REACH
    n_blocks = slab_blocks * n_slab
    tok_f32 = tokens.astype(f32)
    inverse = lax.rsqrt(jnp.mean(tok_f32 * tok_f32, -1, keepdims=True) + norm_eps)
    normed = (tok_f32 * inverse * norm_gain).astype(bf16)
    w_here = lax.dynamic_slice_in_dim(w_qkv, head_index * head_cols, head_cols, 2)
    slab_tok = butterfly_gather(tokens, "head").astype(f32)
    slab_inverse = lax.rsqrt(jnp.mean(slab_tok * slab_tok, -1, keepdims=True) + norm_eps)
    slab_scaled = slab_tok * slab_inverse
    gathered = (slab_scaled * norm_gain).astype(bf16)
    projected = jnp.einsum("rd,cde->cre", gathered, w_here, preferred_element_type=f32)
    packed = jnp.stack(
        [unit_heads(projected[0], head_dim), unit_heads(projected[1], head_dim), projected[2]]
    ).astype(bf16)
    split = lambda value: to_heads(value, slab_blocks, heads_here, head_dim)
    q_heads = split(packed[0])
    keys_values = split(packed[1:])
    extended = padded(keys_values, (("slab", 2),), REACH)
    lookup = (neighbours - slab_index * slab_blocks + REACH) % n_blocks
    choose = lookup[:, :, None] == jnp.arange(ext_blocks, dtype=jnp.int32)
    fetched = jnp.einsum(
        "bse,chekd->chbskd", choose.astype(bf16), extended, preferred_element_type=f32
    ).astype(bf16)
    keys, values = fetched[0], fetched[1]
    live = (jnp.arange(n_slots, dtype=jnp.int32)[None, :] < counts[:, None]).astype(f32)
    scores = exponent_divisor * jnp.einsum(
        "hbqd,hbskd->hbqsk", q_heads, keys, preferred_element_type=f32
    )
    raised = jnp.exp(scores) * live[None, :, None, :, None]
    weights = raised / jnp.sum(raised, (-2, -1), keepdims=True)
    weights_bf = weights.astype(bf16)
    attended_heads = jnp.einsum(
        "hbqsk,hbskd->hbqd", weights_bf, values, preferred_element_type=f32
    ).astype(bf16)
    attended = lax.all_to_all(
        from_heads(attended_heads), "head", split_axis=0, concat_axis=1, tiled=True
    )
    output = (tok_f32 + jnp.dot(attended, w_out, preferred_element_type=f32)).astype(bf16)
    d_out_part = jnp.dot(attended.T, cotangent, preferred_element_type=f32)
    d_attended = jnp.dot(cotangent, w_out.T, preferred_element_type=f32).astype(bf16)
    d_attn = split(lax.all_to_all(d_attended, "head", split_axis=1, concat_axis=0, tiled=True))
    d_weights = jnp.einsum("hbqd,hbskd->hbqsk", d_attn, values, preferred_element_type=f32)
    row_dot = jnp.sum(d_weights * weights, (-2, -1), keepdims=True)
    d_scores = (exponent_divisor * weights * (d_weights - row_dot)).astype(bf16)
    d_query = jnp.einsum("hbqsk,hbskd->hbqd", d_scores, keys, preferred_element_type=f32)
    d_keys = jnp.einsum("hbqsk,hbqd->hbskd", d_scores, q_heads, preferred_element_type=f32)
    d_values = jnp.einsum("hbqsk,hbqd->hbskd", weights_bf, d_attn, preferred_element_type=f32)
    scatter = lambda grads: jnp.einsum(
        "bse,hbskd->hekd",
        choose.astype(f32),
        grads,
        precision=lax.Precision.HIGHEST,
        preferred_element_type=f32,
    )
    grad_ext = jnp.stack([scatter(d_keys), scatter(d_values)])
    low_rim = grad_ext[:, :, :REACH]
    high_rim = grad_ext[:, :, REACH + slab_blocks :]
    from_above = passed_along(low_rim.astype(bf16), "slab", -1).astype(f32)
    from_below = passed_along(high_rim.astype(bf16), "slab", 1).astype(f32)
    own_grads = grad_ext[:, :, REACH : REACH + slab_blocks]
    own_grads = own_grads.at[:, :, slab_blocks - REACH :].add(from_above)
    own_grads = own_grads.at[:, :, :REACH].add(from_below)
    d_packed = jnp.concatenate(
        [from_heads(d_query)[None], from_heads(own_grads)], 0
    ).astype(bf16)
    d_query_part = norm_back(projected[0], d_packed[0], head_dim).astype(bf16)
    d_key_part = norm_back(projected[1], d_packed[1], head_dim).astype(bf16)
    d_qkv = jnp.stack([d_query_part, d_key_part, d_packed[2]])
    d_normed_part = jnp.einsum("crk,cdk->rd", d_qkv, w_here, preferred_element_type=f32)
    d_gain_part = jnp.sum(d_normed_part * slab_scaled, 0)
    shares = d_normed_part.astype(bf16).reshape(n_head, -1, width)
    d_normed = jnp.sum(
        lax.all_to_all(shares, "head", split_axis=0, concat_axis=0, tiled=True).astype(f32), 0
    )
    d_qkv_part = jnp.einsum("rd,crk->cdk", gathered, d_qkv, preferred_element_type=f32)
    slots = jnp.zeros((n_head,) + d_qkv_part.shape, f32)
    slots = lax.dynamic_update_index_in_dim(slots, d_qkv_part, head_index, 0)
    pieces = [slots.reshape(-1, width), d_out_part, d_gain_part[None]]
    rows = sum(piece.shape[0] for piece in pieces)
    n_dev = n_head * n_slab
    pieces.append(jnp.zeros((-rows % n_dev, width), f32))
    total = butterfly_psum(jnp.concatenate(pieces, 0))
    slot_rows = pieces[0].shape[0]
    all_slots = total[:slot_rows].reshape(slots.shape)
    d_w_qkv = lax.dynamic_index_in_dim(all_slots, head_index, 0, keepdims=False)
    d_w_out = total[slot_rows : slot_rows + width]
    d_gain = total[slot_rows + width]
    scaled = d_normed * norm_gain
    d_tokens = (
        cotangent.astype(f32)
        + inverse * scaled
        - tok_f32 * inverse**3 * jnp.mean(scaled * tok_f32, -1, keepdims=True)
    )
    return (output, d_tokens.astype(bf16), d_w_qkv, d_w_out, d_gain)


def solution(mesh):
    placed = (
        P(("slab", "head"), None),
        P(),
        P(),
        P(),
        P(("slab", "head"), None),
        P("slab", None),
        P("slab"),
    )
    return jax.shard_map(
        local,
        mesh=mesh,
        in_specs=placed,
        out_specs=(
            P(("slab", "head"), None),
            P(("slab", "head"), None),
            P(None, None, "head"),
            P(),
            P(),
        ),
        check_vma=False,
    )
```

```python
import math

import jax
import jax.numpy as jnp
from jax import lax
from jax.sharding import PartitionSpec as P

HEADS = 12
BLK = 128
REACH = 16


exponent_divisor = 10.0
norm_eps = 1e-06


def padded(value, sides, width):
    for axis, dim in sides:
        size, length = (lax.axis_size(axis), value.shape[dim])
        up = [(i, (i + 1) % size) for i in range(size)]
        down = [(j, i) for i, j in up]
        last = lax.slice_in_dim(value, length - width, length, axis=dim)
        first = lax.slice_in_dim(value, 0, width, axis=dim)
        before = lax.ppermute(last, axis, up)
        after = lax.ppermute(first, axis, down)
        value = jnp.concatenate([before, value, after], axis=dim)
    return value


def passed_along(value, axis, steps):
    count = lax.axis_size(axis)
    pairs = [(source, (source + steps) % count) for source in range(count)]
    return lax.ppermute(value, axis, pairs)


def normalize(projected, head_dim):
    by_head = projected.reshape(projected.shape[:-1] + (projected.shape[-1] // head_dim, head_dim))
    length = jnp.sqrt(jnp.sum(by_head * by_head, -1, keepdims=True))
    divisor = jnp.maximum(length, 0.7 * math.sqrt(head_dim))
    return (by_head / divisor, divisor, length > 0.7 * math.sqrt(head_dim))


def unit_heads(projected, head_dim):
    unit, divisor, active = normalize(projected, head_dim)
    return unit.reshape(projected.shape)


def norm_back(projected, grad, head_dim):
    unit, divisor, active = normalize(projected, head_dim)
    along = grad.astype(jnp.float32).reshape(unit.shape)
    inner = jnp.sum(unit * along, -1, keepdims=True)
    result = (along - jnp.where(active, unit * inner, 0.0)) / divisor
    return result.reshape(projected.shape)


def xor_steps():
    steps = []
    for axis in ("head", "slab"):
        size = lax.axis_size(axis)
        assert size & (size - 1) == 0
        mask = 1
        while mask < size:
            steps.append((axis, mask))
            mask *= 2
    return steps


def xor_swap(value, axis, mask):
    size = lax.axis_size(axis)
    return lax.ppermute(value, axis, [(i, i ^ mask) for i in range(size)])


def ordered_pair(held, received, bit):
    pair = jnp.stack([held, received])
    first = lax.dynamic_index_in_dim(pair, bit, 0, keepdims=False)
    second = lax.dynamic_index_in_dim(pair, 1 - bit, 0, keepdims=False)
    return jnp.concatenate([first, second], 0)


def butterfly_gather(value, axis):
    size = lax.axis_size(axis)
    held = value
    mask = 1
    while mask < size:
        bit = (lax.axis_index(axis) // mask) % 2
        held = ordered_pair(held, xor_swap(held, axis, mask), bit)
        mask *= 2
    return held


def butterfly_psum(value, wire, tie, tie_step):
    steps = xor_steps()
    held = value
    bits = []
    for index, (axis, mask) in enumerate(steps):
        if index == tie_step:
            held, tie = lax.optimization_barrier((held, tie))
        bit = (lax.axis_index(axis) // mask) % 2
        halves = held.reshape((2, held.shape[0] // 2) + held.shape[1:])
        keep = lax.dynamic_index_in_dim(halves, bit, 0, keepdims=False)
        send = lax.dynamic_index_in_dim(halves, 1 - bit, 0, keepdims=False)
        held = keep + xor_swap(send.astype(wire), axis, mask).astype(value.dtype)
        bits.append(bit)
    held = held.astype(wire)
    for (axis, mask), bit in reversed(list(zip(steps, bits))):
        held = ordered_pair(held, xor_swap(held, axis, mask), bit)
    return held.astype(value.dtype), tie


def to_heads(value, blocks, heads_here, head_dim):
    lead = value.shape[:-2]
    value = value.reshape(lead + (blocks, BLK, heads_here, head_dim))
    return jnp.moveaxis(value, len(lead) + 2, len(lead))


def from_heads(value):
    lead = value.shape[:-4]
    heads_here, blocks, rows, head_dim = value.shape[len(lead) :]
    value = jnp.moveaxis(value, len(lead), len(lead) + 2)
    return value.reshape(lead + (blocks * rows, heads_here * head_dim))


def local(tokens, norm_gain, w_qkv, w_out, cotangent, neighbours, counts):
    f32, bf16 = jnp.float32, jnp.bfloat16
    width = tokens.shape[1]
    head_dim = width // HEADS
    n_head = lax.axis_size("head")
    n_slab = lax.axis_size("slab")
    head_cols = width // n_head
    heads_here = HEADS // n_head
    head_index = lax.axis_index("head")
    slab_index = lax.axis_index("slab")
    slab_blocks, n_slots = neighbours.shape
    ext_blocks = slab_blocks + 2 * REACH
    n_blocks = slab_blocks * n_slab
    tok_f32 = tokens.astype(f32)
    inverse = lax.rsqrt(jnp.mean(tok_f32 * tok_f32, -1, keepdims=True) + norm_eps)
    normed = (tok_f32 * inverse * norm_gain).astype(bf16)
    w_here = lax.dynamic_slice_in_dim(w_qkv, head_index * head_cols, head_cols, 2)
    slab_tok = butterfly_gather(tokens, "head").astype(f32)
    slab_inverse = lax.rsqrt(jnp.mean(slab_tok * slab_tok, -1, keepdims=True) + norm_eps)
    slab_scaled = slab_tok * slab_inverse
    gathered = (slab_scaled * norm_gain).astype(bf16)
    projected = jnp.einsum("rd,cde->cre", gathered, w_here, preferred_element_type=f32)
    packed = jnp.stack(
        [unit_heads(projected[0], head_dim), unit_heads(projected[1], head_dim), projected[2]]
    ).astype(bf16)
    split = lambda value: to_heads(value, slab_blocks, heads_here, head_dim)
    q_heads = split(packed[0])
    lookup = (neighbours - slab_index * slab_blocks + REACH) % n_blocks
    choose = lookup[:, :, None] == jnp.arange(ext_blocks, dtype=jnp.int32)
    fetch = lambda value: jnp.einsum(
        "bse,hekd->hbskd",
        choose.astype(bf16),
        padded(split(value), (("slab", 1),), REACH),
        preferred_element_type=f32,
    ).astype(bf16)
    keys, values = fetch(packed[1]), fetch(packed[2])
    live = (jnp.arange(n_slots, dtype=jnp.int32)[None, :] < counts[:, None]).astype(f32)
    scores = exponent_divisor * jnp.einsum(
        "hbqd,hbskd->hbqsk", q_heads, keys, preferred_element_type=f32
    )
    raised = jnp.exp(scores) * live[None, :, None, :, None]
    weights = raised / jnp.sum(raised, (-2, -1), keepdims=True)
    weights_bf = weights.astype(bf16)
    attended_heads = jnp.einsum(
        "hbqsk,hbskd->hbqd", weights_bf, values, preferred_element_type=f32
    ).astype(bf16)
    attended = lax.all_to_all(
        from_heads(attended_heads), "head", split_axis=0, concat_axis=1, tiled=True
    )
    output = (tok_f32 + jnp.dot(attended, w_out, preferred_element_type=f32)).astype(bf16)
    d_out_part = jnp.dot(attended.T, cotangent, preferred_element_type=f32)
    d_attended = jnp.dot(cotangent, w_out.T, preferred_element_type=f32).astype(bf16)
    d_attn = split(lax.all_to_all(d_attended, "head", split_axis=1, concat_axis=0, tiled=True))
    d_weights = jnp.einsum("hbqd,hbskd->hbqsk", d_attn, values, preferred_element_type=f32)
    row_dot = jnp.sum(d_weights * weights, (-2, -1), keepdims=True)
    d_scores = (exponent_divisor * weights * (d_weights - row_dot)).astype(bf16)
    d_query = jnp.einsum("hbqsk,hbskd->hbqd", d_scores, keys, preferred_element_type=f32)
    d_keys = jnp.einsum("hbqsk,hbqd->hbskd", d_scores, q_heads, preferred_element_type=f32)
    d_values = jnp.einsum("hbqsk,hbqd->hbskd", weights_bf, d_attn, preferred_element_type=f32)
    scatter = lambda grads: jnp.einsum(
        "bse,hbskd->hekd",
        choose.astype(f32),
        grads,
        precision=lax.Precision.HIGHEST,
        preferred_element_type=f32,
    )
    grad_ext = jnp.stack([scatter(d_keys), scatter(d_values)])
    low_rim = grad_ext[:, :, :REACH]
    high_rim = grad_ext[:, :, REACH + slab_blocks :]
    from_above = passed_along(low_rim.astype(bf16), "slab", -1).astype(f32)
    from_below = passed_along(high_rim.astype(bf16), "slab", 1).astype(f32)
    own_grads = grad_ext[:, :, REACH : REACH + slab_blocks]
    own_grads = own_grads.at[:, :, slab_blocks - REACH :].add(from_above)
    own_grads = own_grads.at[:, :, :REACH].add(from_below)
    d_packed = jnp.concatenate(
        [from_heads(d_query)[None], from_heads(own_grads)], 0
    ).astype(bf16)
    d_query_part = norm_back(projected[0], d_packed[0], head_dim).astype(bf16)
    d_key_part = norm_back(projected[1], d_packed[1], head_dim).astype(bf16)
    d_qkv = jnp.stack([d_query_part, d_key_part, d_packed[2]])
    d_normed_part = jnp.einsum("crk,cdk->rd", d_qkv, w_here, preferred_element_type=f32)
    d_gain_part = jnp.sum(d_normed_part * slab_scaled, 0)
    shares = d_normed_part.astype(bf16).reshape(n_head, -1, width)
    received = lax.all_to_all(shares, "head", split_axis=0, concat_axis=0, tiled=True)
    d_qkv_part = jnp.einsum("rd,crk->cdk", gathered, d_qkv, preferred_element_type=f32)
    slots = jnp.zeros((n_head,) + d_qkv_part.shape, f32)
    slots = lax.dynamic_update_index_in_dim(slots, d_qkv_part, head_index, 0)
    pieces = [slots.reshape(-1, width), d_out_part, d_gain_part[None]]
    rows = sum(piece.shape[0] for piece in pieces)
    n_dev = n_head * n_slab
    pieces.append(jnp.zeros((-rows % n_dev, width), f32))
    total, received = butterfly_psum(jnp.concatenate(pieces, 0), bf16, received, 2)
    d_normed = jnp.sum(received.astype(f32), 0)
    slot_rows = pieces[0].shape[0]
    all_slots = total[:slot_rows].reshape(slots.shape)
    d_w_qkv = lax.dynamic_index_in_dim(all_slots, head_index, 0, keepdims=False)
    d_w_out = total[slot_rows : slot_rows + width]
    d_gain = total[slot_rows + width]
    scaled = d_normed * norm_gain
    d_tokens = (
        cotangent.astype(f32)
        + inverse * scaled
        - tok_f32 * inverse**3 * jnp.mean(scaled * tok_f32, -1, keepdims=True)
    )
    return (output, d_tokens.astype(bf16), d_w_qkv, d_w_out, d_gain)


def solution(mesh):
    placed = (
        P(("slab", "head"), None),
        P(),
        P(),
        P(),
        P(("slab", "head"), None),
        P("slab", None),
        P("slab"),
    )
    return jax.shard_map(
        local,
        mesh=mesh,
        in_specs=placed,
        out_specs=(
            P(("slab", "head"), None),
            P(("slab", "head"), None),
            P(None, None, "head"),
            P(),
            P(),
        ),
        check_vma=False,
    )
```

```python
import math

import jax
import jax.numpy as jnp
from jax import lax
from jax.sharding import PartitionSpec as P

HEADS = 12
BLK = 128
REACH = 16


exponent_divisor = 10.0
norm_eps = 1e-06


def padded(value, sides, width):
    for axis, dim in sides:
        size, length = (lax.axis_size(axis), value.shape[dim])
        up = [(i, (i + 1) % size) for i in range(size)]
        down = [(j, i) for i, j in up]
        last = lax.slice_in_dim(value, length - width, length, axis=dim)
        first = lax.slice_in_dim(value, 0, width, axis=dim)
        before = lax.ppermute(last, axis, up)
        after = lax.ppermute(first, axis, down)
        value = jnp.concatenate([before, value, after], axis=dim)
    return value


def passed_along(value, axis, steps):
    count = lax.axis_size(axis)
    pairs = [(source, (source + steps) % count) for source in range(count)]
    return lax.ppermute(value, axis, pairs)


def normalize(projected, head_dim):
    by_head = projected.reshape(projected.shape[:-1] + (projected.shape[-1] // head_dim, head_dim))
    length = jnp.sqrt(jnp.sum(by_head * by_head, -1, keepdims=True))
    divisor = jnp.maximum(length, 0.7 * math.sqrt(head_dim))
    return (by_head / divisor, divisor, length > 0.7 * math.sqrt(head_dim))


def unit_heads(projected, head_dim):
    unit, divisor, active = normalize(projected, head_dim)
    return unit.reshape(projected.shape)


def norm_back(projected, grad, head_dim):
    unit, divisor, active = normalize(projected, head_dim)
    along = grad.astype(jnp.float32).reshape(unit.shape)
    inner = jnp.sum(unit * along, -1, keepdims=True)
    result = (along - jnp.where(active, unit * inner, 0.0)) / divisor
    return result.reshape(projected.shape)


def xor_steps():
    steps = []
    for axis in ("head", "slab"):
        size = lax.axis_size(axis)
        assert size & (size - 1) == 0
        mask = 1
        while mask < size:
            steps.append((axis, mask))
            mask *= 2
    return steps


def xor_swap(value, axis, mask):
    size = lax.axis_size(axis)
    return lax.ppermute(value, axis, [(i, i ^ mask) for i in range(size)])


def ordered_pair(held, received, bit):
    pair = jnp.stack([held, received])
    first = lax.dynamic_index_in_dim(pair, bit, 0, keepdims=False)
    second = lax.dynamic_index_in_dim(pair, 1 - bit, 0, keepdims=False)
    return jnp.concatenate([first, second], 0)


def butterfly_gather(value, axis):
    size = lax.axis_size(axis)
    held = value
    mask = 1
    while mask < size:
        bit = (lax.axis_index(axis) // mask) % 2
        held = ordered_pair(held, xor_swap(held, axis, mask), bit)
        mask *= 2
    return held


def butterfly_psum(value, wire, side_input, side_fn, start_step, join_step):
    steps = xor_steps()
    held = value
    bits = []
    side = None
    for index, (axis, mask) in enumerate(steps):
        if index == start_step:
            held, side_input = lax.optimization_barrier((held, side_input))
            side = side_fn(side_input)
        bit = (lax.axis_index(axis) // mask) % 2
        halves = held.reshape((2, held.shape[0] // 2) + held.shape[1:])
        keep = lax.dynamic_index_in_dim(halves, bit, 0, keepdims=False)
        send = lax.dynamic_index_in_dim(halves, 1 - bit, 0, keepdims=False)
        held = keep + xor_swap(send.astype(wire), axis, mask).astype(value.dtype)
        bits.append(bit)
    held = held.astype(wire)
    for index, ((axis, mask), bit) in enumerate(reversed(list(zip(steps, bits)))):
        if index == join_step:
            held, side = lax.optimization_barrier((held, side))
        held = ordered_pair(held, xor_swap(held, axis, mask), bit)
    return held.astype(value.dtype), side


def to_heads(value, blocks, heads_here, head_dim):
    lead = value.shape[:-2]
    value = value.reshape(lead + (blocks, BLK, heads_here, head_dim))
    return jnp.moveaxis(value, len(lead) + 2, len(lead))


def from_heads(value):
    lead = value.shape[:-4]
    heads_here, blocks, rows, head_dim = value.shape[len(lead) :]
    value = jnp.moveaxis(value, len(lead), len(lead) + 2)
    return value.reshape(lead + (blocks * rows, heads_here * head_dim))


def local(tokens, norm_gain, w_qkv, w_out, cotangent, neighbours, counts):
    f32, bf16 = jnp.float32, jnp.bfloat16
    width = tokens.shape[1]
    head_dim = width // HEADS
    n_head = lax.axis_size("head")
    n_slab = lax.axis_size("slab")
    head_cols = width // n_head
    heads_here = HEADS // n_head
    head_index = lax.axis_index("head")
    slab_index = lax.axis_index("slab")
    slab_blocks, n_slots = neighbours.shape
    ext_blocks = slab_blocks + 2 * REACH
    n_blocks = slab_blocks * n_slab
    tok_f32 = tokens.astype(f32)
    inverse = lax.rsqrt(jnp.mean(tok_f32 * tok_f32, -1, keepdims=True) + norm_eps)
    normed = (tok_f32 * inverse * norm_gain).astype(bf16)
    w_here = lax.dynamic_slice_in_dim(w_qkv, head_index * head_cols, head_cols, 2)
    slab_tok = butterfly_gather(tokens, "head").astype(f32)
    slab_inverse = lax.rsqrt(jnp.mean(slab_tok * slab_tok, -1, keepdims=True) + norm_eps)
    slab_scaled = slab_tok * slab_inverse
    gathered = (slab_scaled * norm_gain).astype(bf16)
    projected = jnp.einsum("rd,cde->cre", gathered, w_here, preferred_element_type=f32)
    packed = jnp.stack(
        [unit_heads(projected[0], head_dim), unit_heads(projected[1], head_dim), projected[2]]
    ).astype(bf16)
    split = lambda value: to_heads(value, slab_blocks, heads_here, head_dim)
    q_heads = split(packed[0])
    lookup = (neighbours - slab_index * slab_blocks + REACH) % n_blocks
    choose = lookup[:, :, None] == jnp.arange(ext_blocks, dtype=jnp.int32)
    fetch = lambda value: jnp.einsum(
        "bse,hekd->hbskd",
        choose.astype(bf16),
        padded(split(value), (("slab", 1),), REACH),
        preferred_element_type=f32,
    ).astype(bf16)
    keys, values = fetch(packed[1]), fetch(packed[2])
    live = (jnp.arange(n_slots, dtype=jnp.int32)[None, :] < counts[:, None]).astype(f32)
    scores = exponent_divisor * jnp.einsum(
        "hbqd,hbskd->hbqsk", q_heads, keys, preferred_element_type=f32
    )
    raised = jnp.exp(scores) * live[None, :, None, :, None]
    weights = raised / jnp.sum(raised, (-2, -1), keepdims=True)
    weights_bf = weights.astype(bf16)
    attended_heads = jnp.einsum(
        "hbqsk,hbskd->hbqd", weights_bf, values, preferred_element_type=f32
    ).astype(bf16)
    attended = lax.all_to_all(
        from_heads(attended_heads), "head", split_axis=0, concat_axis=1, tiled=True
    )
    output = (tok_f32 + jnp.dot(attended, w_out, preferred_element_type=f32)).astype(bf16)
    d_out_part = jnp.dot(attended.T, cotangent, preferred_element_type=f32)
    d_attended = jnp.dot(cotangent, w_out.T, preferred_element_type=f32).astype(bf16)
    d_attended, keys = lax.optimization_barrier((d_attended, keys))
    d_attn = split(lax.all_to_all(d_attended, "head", split_axis=1, concat_axis=0, tiled=True))
    d_weights = jnp.einsum("hbqd,hbskd->hbqsk", d_attn, values, preferred_element_type=f32)
    row_dot = jnp.sum(d_weights * weights, (-2, -1), keepdims=True)
    d_scores = (exponent_divisor * weights * (d_weights - row_dot)).astype(bf16)
    attended, d_scores = lax.optimization_barrier((attended, d_scores))
    d_query = jnp.einsum("hbqsk,hbskd->hbqd", d_scores, keys, preferred_element_type=f32)
    d_keys = jnp.einsum("hbqsk,hbqd->hbskd", d_scores, q_heads, preferred_element_type=f32)
    d_values = jnp.einsum("hbqsk,hbqd->hbskd", weights_bf, d_attn, preferred_element_type=f32)
    scatter = lambda grads: jnp.einsum(
        "bse,hbskd->hekd",
        choose.astype(f32),
        grads,
        precision=lax.Precision.HIGHEST,
        preferred_element_type=f32,
    )
    grad_ext = jnp.stack([scatter(d_keys), scatter(d_values)])
    low_rim = grad_ext[:, :, :REACH]
    high_rim = grad_ext[:, :, REACH + slab_blocks :]
    from_above = passed_along(low_rim.astype(bf16), "slab", -1).astype(f32)
    from_below = passed_along(high_rim.astype(bf16), "slab", 1).astype(f32)
    own_grads = grad_ext[:, :, REACH : REACH + slab_blocks]
    own_grads = own_grads.at[:, :, slab_blocks - REACH :].add(from_above)
    own_grads = own_grads.at[:, :, :REACH].add(from_below)
    d_packed = jnp.concatenate(
        [from_heads(d_query)[None], from_heads(own_grads)], 0
    ).astype(bf16)
    d_query_part = norm_back(projected[0], d_packed[0], head_dim).astype(bf16)
    d_key_part = norm_back(projected[1], d_packed[1], head_dim).astype(bf16)
    d_qkv = jnp.stack([d_query_part, d_key_part, d_packed[2]])
    d_normed_part = jnp.einsum("crk,cdk->rd", d_qkv, w_here, preferred_element_type=f32)
    d_gain_part = jnp.sum(d_normed_part * slab_scaled, 0)
    shares = d_normed_part.astype(bf16).reshape(n_head, -1, width)
    d_qkv_part = jnp.einsum("rd,crk->cdk", gathered, d_qkv, preferred_element_type=f32)
    slots = jnp.zeros((n_head,) + d_qkv_part.shape, f32)
    slots = lax.dynamic_update_index_in_dim(slots, d_qkv_part, head_index, 0)
    pieces = [slots.reshape(-1, width), d_out_part, d_gain_part[None]]
    rows = sum(piece.shape[0] for piece in pieces)
    n_dev = n_head * n_slab
    pieces.append(jnp.zeros((-rows % n_dev, width), f32))
    exchange = lambda value: lax.all_to_all(value, "head", split_axis=0, concat_axis=0, tiled=True)
    head_steps = sum(1 for axis, _ in xor_steps() if axis == "head")
    total, received = butterfly_psum(
        jnp.concatenate(pieces, 0), bf16, shares, exchange, head_steps, 1
    )
    d_normed = jnp.sum(received.astype(f32), 0)
    slot_rows = pieces[0].shape[0]
    all_slots = total[:slot_rows].reshape(slots.shape)
    d_w_qkv = lax.dynamic_index_in_dim(all_slots, head_index, 0, keepdims=False)
    d_w_out = total[slot_rows : slot_rows + width]
    d_gain = total[slot_rows + width]
    scaled = d_normed * norm_gain
    d_tokens = (
        cotangent.astype(f32)
        + inverse * scaled
        - tok_f32 * inverse**3 * jnp.mean(scaled * tok_f32, -1, keepdims=True)
    )
    return (output, d_tokens.astype(bf16), d_w_qkv, d_w_out, d_gain)


def solution(mesh):
    placed = (
        P(("slab", "head"), None),
        P(),
        P(),
        P(),
        P(("slab", "head"), None),
        P("slab", None),
        P("slab"),
    )
    return jax.shard_map(
        local,
        mesh=mesh,
        in_specs=placed,
        out_specs=(
            P(("slab", "head"), None),
            P(("slab", "head"), None),
            P(None, None, "head"),
            P(),
            P(),
        ),
        check_vma=False,
    )
```

```python
import math

import jax
import jax.numpy as jnp
from jax import lax
from jax.sharding import PartitionSpec as P

HEADS = 12
BLK = 128
REACH = 16


exponent_divisor = 10.0
norm_eps = 1e-06


def padded(value, sides, width):
    for axis, dim in sides:
        size, length = (lax.axis_size(axis), value.shape[dim])
        up = [(i, (i + 1) % size) for i in range(size)]
        down = [(j, i) for i, j in up]
        last = lax.slice_in_dim(value, length - width, length, axis=dim)
        first = lax.slice_in_dim(value, 0, width, axis=dim)
        before = lax.ppermute(last, axis, up)
        after = lax.ppermute(first, axis, down)
        value = jnp.concatenate([before, value, after], axis=dim)
    return value


def passed_along(value, axis, steps):
    count = lax.axis_size(axis)
    pairs = [(source, (source + steps) % count) for source in range(count)]
    return lax.ppermute(value, axis, pairs)


def normalize(projected, head_dim):
    by_head = projected.reshape(projected.shape[:-1] + (projected.shape[-1] // head_dim, head_dim))
    length = jnp.sqrt(jnp.sum(by_head * by_head, -1, keepdims=True))
    divisor = jnp.maximum(length, 0.7 * math.sqrt(head_dim))
    return (by_head / divisor, divisor, length > 0.7 * math.sqrt(head_dim))


def unit_heads(projected, head_dim):
    unit, divisor, active = normalize(projected, head_dim)
    return unit.reshape(projected.shape)


def norm_back(projected, grad, head_dim):
    unit, divisor, active = normalize(projected, head_dim)
    along = grad.astype(jnp.float32).reshape(unit.shape)
    inner = jnp.sum(unit * along, -1, keepdims=True)
    result = (along - jnp.where(active, unit * inner, 0.0)) / divisor
    return result.reshape(projected.shape)


def xor_steps(axes):
    steps = []
    for axis in axes:
        size = lax.axis_size(axis)
        assert size & (size - 1) == 0
        mask = 1
        while mask < size:
            steps.append((axis, mask))
            mask *= 2
    return steps


def xor_swap(value, axis, mask):
    size = lax.axis_size(axis)
    return lax.ppermute(value, axis, [(i, i ^ mask) for i in range(size)])


def ordered_pair(held, received, bit):
    pair = jnp.stack([held, received])
    first = lax.dynamic_index_in_dim(pair, bit, 0, keepdims=False)
    second = lax.dynamic_index_in_dim(pair, 1 - bit, 0, keepdims=False)
    return jnp.concatenate([first, second], 0)


def butterfly_gather(value, axis):
    size = lax.axis_size(axis)
    held = value
    mask = 1
    while mask < size:
        bit = (lax.axis_index(axis) // mask) % 2
        held = ordered_pair(held, xor_swap(held, axis, mask), bit)
        mask *= 2
    return held


def scatter_steps(held, steps, wire):
    bits = []
    for axis, mask in steps:
        bit = (lax.axis_index(axis) // mask) % 2
        halves = held.reshape((2, held.shape[0] // 2) + held.shape[1:])
        keep = lax.dynamic_index_in_dim(halves, bit, 0, keepdims=False)
        send = lax.dynamic_index_in_dim(halves, 1 - bit, 0, keepdims=False)
        held = keep + xor_swap(send.astype(wire), axis, mask).astype(held.dtype)
        bits.append(bit)
    return held, bits


def gather_steps(held, steps, bits):
    for (axis, mask), bit in reversed(list(zip(steps, bits))):
        held = ordered_pair(held, xor_swap(held, axis, mask), bit)
    return held


def pad_rows(value, multiple):
    return jnp.concatenate(
        [value, jnp.zeros((-value.shape[0] % multiple,) + value.shape[1:], value.dtype)], 0
    )


def to_heads(value, blocks, heads_here, head_dim):
    lead = value.shape[:-2]
    value = value.reshape(lead + (blocks, BLK, heads_here, head_dim))
    return jnp.moveaxis(value, len(lead) + 2, len(lead))


def from_heads(value):
    lead = value.shape[:-4]
    heads_here, blocks, rows, head_dim = value.shape[len(lead) :]
    value = jnp.moveaxis(value, len(lead), len(lead) + 2)
    return value.reshape(lead + (blocks * rows, heads_here * head_dim))


def local(tokens, norm_gain, w_qkv, w_out, cotangent, neighbours, counts):
    f32, bf16 = jnp.float32, jnp.bfloat16
    width = tokens.shape[1]
    head_dim = width // HEADS
    n_head = lax.axis_size("head")
    n_slab = lax.axis_size("slab")
    head_cols = width // n_head
    heads_here = HEADS // n_head
    head_index = lax.axis_index("head")
    slab_index = lax.axis_index("slab")
    slab_blocks, n_slots = neighbours.shape
    ext_blocks = slab_blocks + 2 * REACH
    n_blocks = slab_blocks * n_slab
    tok_f32 = tokens.astype(f32)
    inverse = lax.rsqrt(jnp.mean(tok_f32 * tok_f32, -1, keepdims=True) + norm_eps)
    normed = (tok_f32 * inverse * norm_gain).astype(bf16)
    w_here = lax.dynamic_slice_in_dim(w_qkv, head_index * head_cols, head_cols, 2)
    slab_tok = butterfly_gather(tokens, "head").astype(f32)
    slab_inverse = lax.rsqrt(jnp.mean(slab_tok * slab_tok, -1, keepdims=True) + norm_eps)
    slab_scaled = slab_tok * slab_inverse
    gathered = (slab_scaled * norm_gain).astype(bf16)
    projected = jnp.einsum("rd,cde->cre", gathered, w_here, preferred_element_type=f32)
    packed = jnp.stack(
        [unit_heads(projected[0], head_dim), unit_heads(projected[1], head_dim), projected[2]]
    ).astype(bf16)
    split = lambda value: to_heads(value, slab_blocks, heads_here, head_dim)
    q_heads = split(packed[0])
    lookup = (neighbours - slab_index * slab_blocks + REACH) % n_blocks
    choose = lookup[:, :, None] == jnp.arange(ext_blocks, dtype=jnp.int32)
    fetch = lambda value: jnp.einsum(
        "bse,hekd->hbskd",
        choose.astype(bf16),
        padded(split(value), (("slab", 1),), REACH),
        preferred_element_type=f32,
    ).astype(bf16)
    keys, values = fetch(packed[1]), fetch(packed[2])
    live = (jnp.arange(n_slots, dtype=jnp.int32)[None, :] < counts[:, None]).astype(f32)
    scores = exponent_divisor * jnp.einsum(
        "hbqd,hbskd->hbqsk", q_heads, keys, preferred_element_type=f32
    )
    raised = jnp.exp(scores) * live[None, :, None, :, None]
    weights = raised / jnp.sum(raised, (-2, -1), keepdims=True)
    weights_bf = weights.astype(bf16)
    attended_heads = jnp.einsum(
        "hbqsk,hbskd->hbqd", weights_bf, values, preferred_element_type=f32
    ).astype(bf16)
    attended = lax.all_to_all(
        from_heads(attended_heads), "head", split_axis=0, concat_axis=1, tiled=True
    )
    output = (tok_f32 + jnp.dot(attended, w_out, preferred_element_type=f32)).astype(bf16)
    d_out_part = jnp.dot(attended.T, cotangent, preferred_element_type=f32)
    d_attended = jnp.dot(cotangent, w_out.T, preferred_element_type=f32).astype(bf16)
    d_attended, keys = lax.optimization_barrier((d_attended, keys))
    d_attn = split(lax.all_to_all(d_attended, "head", split_axis=1, concat_axis=0, tiled=True))
    d_weights = jnp.einsum("hbqd,hbskd->hbqsk", d_attn, values, preferred_element_type=f32)
    row_dot = jnp.sum(d_weights * weights, (-2, -1), keepdims=True)
    d_scores = (exponent_divisor * weights * (d_weights - row_dot)).astype(bf16)
    attended, d_scores = lax.optimization_barrier((attended, d_scores))
    d_query = jnp.einsum("hbqsk,hbskd->hbqd", d_scores, keys, preferred_element_type=f32)
    d_keys = jnp.einsum("hbqsk,hbqd->hbskd", d_scores, q_heads, preferred_element_type=f32)
    d_values = jnp.einsum("hbqsk,hbqd->hbskd", weights_bf, d_attn, preferred_element_type=f32)
    scatter = lambda grads: jnp.einsum(
        "bse,hbskd->hekd",
        choose.astype(f32),
        grads,
        precision=lax.Precision.HIGH,
        preferred_element_type=f32,
    )
    grad_ext = jnp.stack([scatter(d_keys), scatter(d_values)])
    low_rim = grad_ext[:, :, :REACH]
    high_rim = grad_ext[:, :, REACH + slab_blocks :]
    from_above = passed_along(low_rim.astype(bf16), "slab", -1).astype(f32)
    from_below = passed_along(high_rim.astype(bf16), "slab", 1).astype(f32)
    own_grads = grad_ext[:, :, REACH : REACH + slab_blocks]
    own_grads = own_grads.at[:, :, slab_blocks - REACH :].add(from_above)
    own_grads = own_grads.at[:, :, :REACH].add(from_below)
    d_packed = jnp.concatenate(
        [from_heads(d_query)[None], from_heads(own_grads)], 0
    ).astype(bf16)
    d_query_part = norm_back(projected[0], d_packed[0], head_dim).astype(bf16)
    d_key_part = norm_back(projected[1], d_packed[1], head_dim).astype(bf16)
    d_qkv = jnp.stack([d_query_part, d_key_part, d_packed[2]])
    d_normed_part = jnp.einsum("crk,cdk->rd", d_qkv, w_here, preferred_element_type=f32)
    d_gain_part = jnp.sum(d_normed_part * slab_scaled, 0)
    shares = d_normed_part.astype(bf16).reshape(n_head, -1, width)
    d_qkv_part = jnp.einsum("rd,crk->cdk", gathered, d_qkv, preferred_element_type=f32)
    head_steps, slab_steps = xor_steps(("head",)), xor_steps(("slab",))
    sub = 8
    wide = pad_rows(jnp.concatenate([d_out_part, d_gain_part[None]], 0), n_head * sub)
    wide_part, head_bits = scatter_steps(wide, head_steps, bf16)
    wide_part, shares = lax.optimization_barrier((wide_part, shares))
    received = lax.all_to_all(shares, "head", split_axis=0, concat_axis=0, tiled=True)
    narrow = d_qkv_part.reshape(-1, width)
    both = pad_rows(jnp.concatenate([narrow, wide_part], 0), n_slab)
    both_part, slab_bits = scatter_steps(both, slab_steps, bf16)
    both = gather_steps(both_part.astype(bf16), slab_steps, slab_bits)
    narrow_rows = narrow.shape[0]
    wide_part = both[narrow_rows : narrow_rows + wide_part.shape[0]]
    wide_part, received = lax.optimization_barrier((wide_part, received))
    wide = gather_steps(wide_part, head_steps, head_bits).astype(f32)
    d_w_qkv = both[:narrow_rows].astype(f32).reshape(d_qkv_part.shape)
    d_w_out = wide[:width]
    d_gain = wide[width]
    d_normed = jnp.sum(received.astype(f32), 0)
    scaled = d_normed * norm_gain
    d_tokens = (
        cotangent.astype(f32)
        + inverse * scaled
        - tok_f32 * inverse**3 * jnp.mean(scaled * tok_f32, -1, keepdims=True)
    )
    return (output, d_tokens.astype(bf16), d_w_qkv, d_w_out, d_gain)


def solution(mesh):
    placed = (
        P(("slab", "head"), None),
        P(),
        P(),
        P(),
        P(("slab", "head"), None),
        P("slab", None),
        P("slab"),
    )
    return jax.shard_map(
        local,
        mesh=mesh,
        in_specs=placed,
        out_specs=(
            P(("slab", "head"), None),
            P(("slab", "head"), None),
            P(None, None, "head"),
            P(),
            P(),
        ),
        check_vma=False,
    )
```

```python
import math

import jax
import jax.numpy as jnp
from jax import lax
from jax.sharding import PartitionSpec as P

HEADS = 12
BLK = 128
REACH = 16


exponent_divisor = 10.0
norm_eps = 1e-06


def padded(value, sides, width):
    for axis, dim in sides:
        size, length = (lax.axis_size(axis), value.shape[dim])
        up = [(i, (i + 1) % size) for i in range(size)]
        down = [(j, i) for i, j in up]
        last = lax.slice_in_dim(value, length - width, length, axis=dim)
        first = lax.slice_in_dim(value, 0, width, axis=dim)
        before = lax.ppermute(last, axis, up)
        after = lax.ppermute(first, axis, down)
        value = jnp.concatenate([before, value, after], axis=dim)
    return value


def passed_along(value, axis, steps):
    count = lax.axis_size(axis)
    pairs = [(source, (source + steps) % count) for source in range(count)]
    return lax.ppermute(value, axis, pairs)


def normalize(projected, head_dim):
    by_head = projected.reshape(projected.shape[:-1] + (projected.shape[-1] // head_dim, head_dim))
    length = jnp.sqrt(jnp.sum(by_head * by_head, -1, keepdims=True))
    divisor = jnp.maximum(length, 0.7 * math.sqrt(head_dim))
    return (by_head / divisor, divisor, length > 0.7 * math.sqrt(head_dim))


def unit_heads(projected, head_dim):
    unit, divisor, active = normalize(projected, head_dim)
    return unit.reshape(projected.shape)


def norm_back(projected, grad, head_dim):
    unit, divisor, active = normalize(projected, head_dim)
    along = grad.astype(jnp.float32).reshape(unit.shape)
    inner = jnp.sum(unit * along, -1, keepdims=True)
    result = (along - jnp.where(active, unit * inner, 0.0)) / divisor
    return result.reshape(projected.shape)


def xor_steps(axes):
    steps = []
    for axis in axes:
        size = lax.axis_size(axis)
        assert size & (size - 1) == 0
        mask = 1
        while mask < size:
            steps.append((axis, mask))
            mask *= 2
    return steps


def xor_swap(value, axis, mask):
    size = lax.axis_size(axis)
    return lax.ppermute(value, axis, [(i, i ^ mask) for i in range(size)])


def ordered_pair(held, received, bit):
    pair = jnp.stack([held, received])
    first = lax.dynamic_index_in_dim(pair, bit, 0, keepdims=False)
    second = lax.dynamic_index_in_dim(pair, 1 - bit, 0, keepdims=False)
    return jnp.concatenate([first, second], 0)


def butterfly_gather(value, axis):
    masks = [mask for _, mask in xor_steps((axis,))][::-1]
    held = value
    for mask in masks:
        bit = (lax.axis_index(axis) // mask) % 2
        held = ordered_pair(held, xor_swap(held, axis, mask), bit)
    depth = len(masks)
    held = held.reshape((2,) * depth + value.shape)
    held = jnp.transpose(held, tuple(range(depth))[::-1] + tuple(range(depth, held.ndim)))
    return held.reshape((-1,) + value.shape[1:])


def scatter_steps(held, steps, wire):
    bits = []
    for axis, mask in steps:
        bit = (lax.axis_index(axis) // mask) % 2
        halves = held.reshape((2, held.shape[0] // 2) + held.shape[1:])
        keep = lax.dynamic_index_in_dim(halves, bit, 0, keepdims=False)
        send = lax.dynamic_index_in_dim(halves, 1 - bit, 0, keepdims=False)
        held = keep + xor_swap(send.astype(wire), axis, mask).astype(held.dtype)
        bits.append(bit)
    return held, bits


def gather_steps(held, steps, bits):
    for (axis, mask), bit in reversed(list(zip(steps, bits))):
        held = ordered_pair(held, xor_swap(held, axis, mask), bit)
    return held


def pad_rows(value, multiple):
    return jnp.concatenate(
        [value, jnp.zeros((-value.shape[0] % multiple,) + value.shape[1:], value.dtype)], 0
    )


def to_heads(value, blocks, heads_here, head_dim):
    lead = value.shape[:-2]
    value = value.reshape(lead + (blocks, BLK, heads_here, head_dim))
    return jnp.moveaxis(value, len(lead) + 2, len(lead))


def from_heads(value):
    lead = value.shape[:-4]
    heads_here, blocks, rows, head_dim = value.shape[len(lead) :]
    value = jnp.moveaxis(value, len(lead), len(lead) + 2)
    return value.reshape(lead + (blocks * rows, heads_here * head_dim))


def local(tokens, norm_gain, w_qkv, w_out, cotangent, neighbours, counts):
    f32, bf16 = jnp.float32, jnp.bfloat16
    width = tokens.shape[1]
    head_dim = width // HEADS
    n_head = lax.axis_size("head")
    n_slab = lax.axis_size("slab")
    head_cols = width // n_head
    heads_here = HEADS // n_head
    head_index = lax.axis_index("head")
    slab_index = lax.axis_index("slab")
    slab_blocks, n_slots = neighbours.shape
    ext_blocks = slab_blocks + 2 * REACH
    n_blocks = slab_blocks * n_slab
    tok_f32 = tokens.astype(f32)
    inverse = lax.rsqrt(jnp.mean(tok_f32 * tok_f32, -1, keepdims=True) + norm_eps)
    normed = (tok_f32 * inverse * norm_gain).astype(bf16)
    w_here = lax.dynamic_slice_in_dim(w_qkv, head_index * head_cols, head_cols, 2)
    slab_tok = butterfly_gather(tokens, "head").astype(f32)
    slab_inverse = lax.rsqrt(jnp.mean(slab_tok * slab_tok, -1, keepdims=True) + norm_eps)
    slab_scaled = slab_tok * slab_inverse
    gathered = (slab_scaled * norm_gain).astype(bf16)
    projected = jnp.einsum("rd,cde->cre", gathered, w_here, preferred_element_type=f32)
    packed = jnp.stack(
        [unit_heads(projected[0], head_dim), unit_heads(projected[1], head_dim), projected[2]]
    ).astype(bf16)
    split = lambda value: to_heads(value, slab_blocks, heads_here, head_dim)
    q_heads = split(packed[0])
    lookup = (neighbours - slab_index * slab_blocks + REACH) % n_blocks
    choose = lookup[:, :, None] == jnp.arange(ext_blocks, dtype=jnp.int32)
    fetch = lambda value: jnp.einsum(
        "bse,hekd->hbskd",
        choose.astype(bf16),
        padded(split(value), (("slab", 1),), REACH),
        preferred_element_type=f32,
    ).astype(bf16)
    keys, values = fetch(packed[1]), fetch(packed[2])
    live = (jnp.arange(n_slots, dtype=jnp.int32)[None, :] < counts[:, None]).astype(f32)
    scores = exponent_divisor * jnp.einsum(
        "hbqd,hbskd->hbqsk", q_heads, keys, preferred_element_type=f32
    )
    raised = jnp.exp(scores) * live[None, :, None, :, None]
    weights = raised / jnp.sum(raised, (-2, -1), keepdims=True)
    weights_bf = weights.astype(bf16)
    attended_heads = jnp.einsum(
        "hbqsk,hbskd->hbqd", weights_bf, values, preferred_element_type=f32
    ).astype(bf16)
    attended = lax.all_to_all(
        from_heads(attended_heads), "head", split_axis=0, concat_axis=1, tiled=True
    )
    output = (tok_f32 + jnp.dot(attended, w_out, preferred_element_type=f32)).astype(bf16)
    d_out_part = jnp.dot(attended.T, cotangent, preferred_element_type=f32)
    d_attended = jnp.dot(cotangent, w_out.T, preferred_element_type=f32).astype(bf16)
    d_attended, keys = lax.optimization_barrier((d_attended, keys))
    d_attn = split(lax.all_to_all(d_attended, "head", split_axis=1, concat_axis=0, tiled=True))
    d_weights = jnp.einsum("hbqd,hbskd->hbqsk", d_attn, values, preferred_element_type=f32)
    row_dot = jnp.sum(d_weights * weights, (-2, -1), keepdims=True)
    d_scores = (exponent_divisor * weights * (d_weights - row_dot)).astype(bf16)
    attended, d_scores = lax.optimization_barrier((attended, d_scores))
    d_query = jnp.einsum("hbqsk,hbskd->hbqd", d_scores, keys, preferred_element_type=f32)
    d_keys = jnp.einsum("hbqsk,hbqd->hbskd", d_scores, q_heads, preferred_element_type=f32)
    d_values = jnp.einsum("hbqsk,hbqd->hbskd", weights_bf, d_attn, preferred_element_type=f32)
    scatter = lambda grads: jnp.einsum(
        "bse,hbskd->hekd",
        choose.astype(f32),
        grads,
        precision=lax.Precision.HIGH,
        preferred_element_type=f32,
    )
    grad_ext = jnp.stack([scatter(d_keys), scatter(d_values)])
    low_rim = grad_ext[:, :, :REACH]
    high_rim = grad_ext[:, :, REACH + slab_blocks :]
    from_above = passed_along(low_rim.astype(bf16), "slab", -1).astype(f32)
    from_below = passed_along(high_rim.astype(bf16), "slab", 1).astype(f32)
    own_grads = grad_ext[:, :, REACH : REACH + slab_blocks]
    own_grads = own_grads.at[:, :, slab_blocks - REACH :].add(from_above)
    own_grads = own_grads.at[:, :, :REACH].add(from_below)
    d_packed = jnp.concatenate(
        [from_heads(d_query)[None], from_heads(own_grads)], 0
    ).astype(bf16)
    d_query_part = norm_back(projected[0], d_packed[0], head_dim).astype(bf16)
    d_key_part = norm_back(projected[1], d_packed[1], head_dim).astype(bf16)
    d_qkv = jnp.stack([d_query_part, d_key_part, d_packed[2]])
    d_normed_part = jnp.einsum("crk,cdk->rd", d_qkv, w_here, preferred_element_type=f32)
    d_gain_part = jnp.sum(d_normed_part * slab_scaled, 0)
    shares = d_normed_part.astype(bf16).reshape(n_head, -1, width)
    d_qkv_part = jnp.einsum("rd,crk->cdk", gathered, d_qkv, preferred_element_type=f32)
    head_steps, slab_steps = xor_steps(("head",)), xor_steps(("slab",))
    sub = 8
    wide = pad_rows(jnp.concatenate([d_out_part, d_gain_part[None]], 0), n_head * sub)
    wide_part, head_bits = scatter_steps(wide, head_steps, bf16)
    wide_part, shares = lax.optimization_barrier((wide_part, shares))
    received = lax.all_to_all(shares, "head", split_axis=0, concat_axis=0, tiled=True)
    narrow = d_qkv_part.reshape(-1, width)
    both = pad_rows(jnp.concatenate([narrow, wide_part], 0), n_slab)
    both_part, slab_bits = scatter_steps(both, slab_steps, bf16)
    both_part, received = lax.optimization_barrier((both_part, received))
    both = gather_steps(both_part.astype(bf16), slab_steps, slab_bits)
    narrow_rows = narrow.shape[0]
    wide_part = both[narrow_rows : narrow_rows + wide_part.shape[0]]
    wide = gather_steps(wide_part, head_steps, head_bits).astype(f32)
    d_w_qkv = both[:narrow_rows].astype(f32).reshape(d_qkv_part.shape)
    d_w_out = wide[:width]
    d_gain = wide[width]
    d_normed = jnp.sum(received.astype(f32), 0)
    scaled = d_normed * norm_gain
    d_tokens = (
        cotangent.astype(f32)
        + inverse * scaled
        - tok_f32 * inverse**3 * jnp.mean(scaled * tok_f32, -1, keepdims=True)
    )
    return (output, d_tokens.astype(bf16), d_w_qkv, d_w_out, d_gain)


def solution(mesh):
    placed = (
        P(("slab", "head"), None),
        P(),
        P(),
        P(),
        P(("slab", "head"), None),
        P("slab", None),
        P("slab"),
    )
    return jax.shard_map(
        local,
        mesh=mesh,
        in_specs=placed,
        out_specs=(
            P(("slab", "head"), None),
            P(("slab", "head"), None),
            P(None, None, "head"),
            P(),
            P(),
        ),
        check_vma=False,
    )
```

```python
import math

import jax
import jax.numpy as jnp
from jax import lax
from jax.sharding import PartitionSpec as P

HEADS = 12
BLK = 128
REACH = 16


exponent_divisor = 10.0
norm_eps = 1e-06


def padded(value, sides, width):
    for axis, dim in sides:
        size, length = (lax.axis_size(axis), value.shape[dim])
        up = [(i, (i + 1) % size) for i in range(size)]
        down = [(j, i) for i, j in up]
        last = lax.slice_in_dim(value, length - width, length, axis=dim)
        first = lax.slice_in_dim(value, 0, width, axis=dim)
        before = lax.ppermute(last, axis, up)
        after = lax.ppermute(first, axis, down)
        value = jnp.concatenate([before, value, after], axis=dim)
    return value


def passed_along(value, axis, steps):
    count = lax.axis_size(axis)
    pairs = [(source, (source + steps) % count) for source in range(count)]
    return lax.ppermute(value, axis, pairs)


def normalize(projected, head_dim):
    by_head = projected.reshape(projected.shape[:-1] + (projected.shape[-1] // head_dim, head_dim))
    length = jnp.sqrt(jnp.sum(by_head * by_head, -1, keepdims=True))
    divisor = jnp.maximum(length, 0.7 * math.sqrt(head_dim))
    return (by_head / divisor, divisor, length > 0.7 * math.sqrt(head_dim))


def unit_heads(projected, head_dim):
    unit, divisor, active = normalize(projected, head_dim)
    return unit.reshape(projected.shape)


def norm_back(projected, grad, head_dim):
    unit, divisor, active = normalize(projected, head_dim)
    along = grad.astype(jnp.float32).reshape(unit.shape)
    inner = jnp.sum(unit * along, -1, keepdims=True)
    result = (along - jnp.where(active, unit * inner, 0.0)) / divisor
    return result.reshape(projected.shape)


def xor_steps(axes):
    steps = []
    for axis in axes:
        size = lax.axis_size(axis)
        assert size & (size - 1) == 0
        mask = 1
        while mask < size:
            steps.append((axis, mask))
            mask *= 2
    return steps


def xor_swap(value, axis, mask):
    size = lax.axis_size(axis)
    return lax.ppermute(value, axis, [(i, i ^ mask) for i in range(size)])


def ordered_pair(held, received, bit):
    pair = jnp.stack([held, received])
    first = lax.dynamic_index_in_dim(pair, bit, 0, keepdims=False)
    second = lax.dynamic_index_in_dim(pair, 1 - bit, 0, keepdims=False)
    return jnp.concatenate([first, second], 0)


def butterfly_gather(value, axis):
    masks = [mask for _, mask in xor_steps((axis,))][::-1]
    held = value
    for mask in masks:
        bit = (lax.axis_index(axis) // mask) % 2
        held = ordered_pair(held, xor_swap(held, axis, mask), bit)
    depth = len(masks)
    held = held.reshape((2,) * depth + value.shape)
    held = jnp.transpose(held, tuple(range(depth))[::-1] + tuple(range(depth, held.ndim)))
    return held.reshape((-1,) + value.shape[1:])


def scatter_steps(held, steps, wire):
    bits = []
    for axis, mask in steps:
        bit = (lax.axis_index(axis) // mask) % 2
        halves = held.reshape((2, held.shape[0] // 2) + held.shape[1:])
        keep = lax.dynamic_index_in_dim(halves, bit, 0, keepdims=False)
        send = lax.dynamic_index_in_dim(halves, 1 - bit, 0, keepdims=False)
        held = keep + xor_swap(send.astype(wire), axis, mask).astype(held.dtype)
        bits.append(bit)
    return held, bits


def gather_steps(held, steps, bits):
    for (axis, mask), bit in reversed(list(zip(steps, bits))):
        held = ordered_pair(held, xor_swap(held, axis, mask), bit)
    return held


def pad_rows(value, multiple):
    return jnp.concatenate(
        [value, jnp.zeros((-value.shape[0] % multiple,) + value.shape[1:], value.dtype)], 0
    )


def to_heads(value, blocks, heads_here, head_dim):
    lead = value.shape[:-2]
    value = value.reshape(lead + (blocks, BLK, heads_here, head_dim))
    return jnp.moveaxis(value, len(lead) + 2, len(lead))


def from_heads(value):
    lead = value.shape[:-4]
    heads_here, blocks, rows, head_dim = value.shape[len(lead) :]
    value = jnp.moveaxis(value, len(lead), len(lead) + 2)
    return value.reshape(lead + (blocks * rows, heads_here * head_dim))


def local(tokens, norm_gain, w_qkv, w_out, cotangent, neighbours, counts):
    f32, bf16 = jnp.float32, jnp.bfloat16
    width = tokens.shape[1]
    head_dim = width // HEADS
    n_head = lax.axis_size("head")
    n_slab = lax.axis_size("slab")
    head_cols = width // n_head
    heads_here = HEADS // n_head
    head_index = lax.axis_index("head")
    slab_index = lax.axis_index("slab")
    slab_blocks, n_slots = neighbours.shape
    ext_blocks = slab_blocks + 2 * REACH
    n_blocks = slab_blocks * n_slab
    tok_f32 = tokens.astype(f32)
    inverse = lax.rsqrt(jnp.mean(tok_f32 * tok_f32, -1, keepdims=True) + norm_eps)
    normed = (tok_f32 * inverse * norm_gain).astype(bf16)
    w_here = lax.dynamic_slice_in_dim(w_qkv, head_index * head_cols, head_cols, 2)
    slab_tok = butterfly_gather(tokens, "head").astype(f32)
    slab_inverse = lax.rsqrt(jnp.mean(slab_tok * slab_tok, -1, keepdims=True) + norm_eps)
    slab_scaled = slab_tok * slab_inverse
    gathered = (slab_scaled * norm_gain).astype(bf16)
    projected = jnp.einsum("rd,cde->cre", gathered, w_here, preferred_element_type=f32)
    packed = jnp.stack(
        [unit_heads(projected[0], head_dim), unit_heads(projected[1], head_dim), projected[2]]
    ).astype(bf16)
    split = lambda value: to_heads(value, slab_blocks, heads_here, head_dim)
    q_heads = split(packed[0])
    lookup = (neighbours - slab_index * slab_blocks + REACH) % n_blocks
    choose = lookup[:, :, None] == jnp.arange(ext_blocks, dtype=jnp.int32)
    fetch = lambda value: jnp.einsum(
        "bse,hekd->hbskd",
        choose.astype(bf16),
        padded(split(value), (("slab", 1),), REACH),
        preferred_element_type=f32,
    ).astype(bf16)
    keys, values = fetch(packed[1]), fetch(packed[2])
    live = (jnp.arange(n_slots, dtype=jnp.int32)[None, :] < counts[:, None]).astype(f32)
    scores = exponent_divisor * jnp.einsum(
        "hbqd,hbskd->hbqsk", q_heads, keys, preferred_element_type=f32
    )
    raised = jnp.exp(scores) * live[None, :, None, :, None]
    weights = raised / jnp.sum(raised, (-2, -1), keepdims=True)
    weights_bf = weights.astype(bf16)
    attended_heads = jnp.einsum(
        "hbqsk,hbskd->hbqd", weights_bf, values, preferred_element_type=f32
    ).astype(bf16)
    attended = lax.all_to_all(
        from_heads(attended_heads), "head", split_axis=0, concat_axis=1, tiled=True
    )
    output = (tok_f32 + jnp.dot(attended, w_out, preferred_element_type=f32)).astype(bf16)
    d_out_part = jnp.dot(attended.T, cotangent, preferred_element_type=f32)
    d_attended = jnp.dot(cotangent, w_out.T, preferred_element_type=f32).astype(bf16)
    d_attended, keys = lax.optimization_barrier((d_attended, keys))
    d_attn = split(lax.all_to_all(d_attended, "head", split_axis=1, concat_axis=0, tiled=True))
    d_weights = jnp.einsum("hbqd,hbskd->hbqsk", d_attn, values, preferred_element_type=f32)
    row_dot = jnp.sum(d_weights * weights, (-2, -1), keepdims=True)
    d_scores = (exponent_divisor * weights * (d_weights - row_dot)).astype(bf16)
    attended, d_scores = lax.optimization_barrier((attended, d_scores))
    d_query = jnp.einsum("hbqsk,hbskd->hbqd", d_scores, keys, preferred_element_type=f32)
    d_keys = jnp.einsum("hbqsk,hbqd->hbskd", d_scores, q_heads, preferred_element_type=f32)
    d_values = jnp.einsum("hbqsk,hbqd->hbskd", weights_bf, d_attn, preferred_element_type=f32)
    scatter = lambda grads: jnp.einsum(
        "bse,hbskd->hekd",
        choose.astype(f32),
        grads,
        precision=lax.Precision.HIGH,
        preferred_element_type=f32,
    )
    grad_ext = jnp.stack([scatter(d_keys), scatter(d_values)])
    low_rim = grad_ext[:, :, :REACH]
    high_rim = grad_ext[:, :, REACH + slab_blocks :]
    from_above = passed_along(low_rim.astype(bf16), "slab", -1).astype(f32)
    from_below = passed_along(high_rim.astype(bf16), "slab", 1).astype(f32)
    own_grads = grad_ext[:, :, REACH : REACH + slab_blocks]
    own_grads = own_grads.at[:, :, slab_blocks - REACH :].add(from_above)
    own_grads = own_grads.at[:, :, :REACH].add(from_below)
    d_packed = jnp.concatenate(
        [from_heads(d_query)[None], from_heads(own_grads)], 0
    ).astype(bf16)
    d_query_part = norm_back(projected[0], d_packed[0], head_dim).astype(bf16)
    d_key_part = norm_back(projected[1], d_packed[1], head_dim).astype(bf16)
    d_qkv = jnp.stack([d_query_part, d_key_part, d_packed[2]])
    d_normed_part = jnp.einsum("crk,cdk->rd", d_qkv, w_here, preferred_element_type=f32)
    d_gain_part = jnp.sum(d_normed_part * slab_scaled, 0)
    shares = d_normed_part.astype(bf16).reshape(n_head, -1, width)
    d_qkv_part = jnp.einsum("rd,crk->cdk", gathered, d_qkv, preferred_element_type=f32)
    head_steps, slab_steps = xor_steps(("head",)), xor_steps(("slab",))
    sub = 8
    wide = pad_rows(jnp.concatenate([d_out_part, d_gain_part[None]], 0), n_head * sub)
    wide_part, head_bits = scatter_steps(wide, head_steps, bf16)
    wide_part, shares = lax.optimization_barrier((wide_part, shares))
    received = lax.all_to_all(shares, "head", split_axis=0, concat_axis=0, tiled=True)
    narrow = d_qkv_part.reshape(-1, width)
    both = pad_rows(jnp.concatenate([narrow, wide_part], 0), n_slab)
    both_part, slab_bits = scatter_steps(both, slab_steps, bf16)
    both = gather_steps(both_part.astype(bf16), slab_steps, slab_bits)
    narrow_rows = narrow.shape[0]
    wide_part = both[narrow_rows : narrow_rows + wide_part.shape[0]]
    wide = gather_steps(wide_part, head_steps, head_bits).astype(f32)
    d_w_qkv = both[:narrow_rows].astype(f32).reshape(d_qkv_part.shape)
    d_w_out = wide[:width]
    d_gain = wide[width]
    d_normed = jnp.sum(received.astype(f32), 0)
    scaled = d_normed * norm_gain
    d_tokens = (
        cotangent.astype(f32)
        + inverse * scaled
        - tok_f32 * inverse**3 * jnp.mean(scaled * tok_f32, -1, keepdims=True)
    )
    return (output, d_tokens.astype(bf16), d_w_qkv, d_w_out, d_gain)


def solution(mesh):
    placed = (
        P(("slab", "head"), None),
        P(),
        P(),
        P(),
        P(("slab", "head"), None),
        P("slab", None),
        P("slab"),
    )
    return jax.shard_map(
        local,
        mesh=mesh,
        in_specs=placed,
        out_specs=(
            P(("slab", "head"), None),
            P(("slab", "head"), None),
            P(None, None, "head"),
            P(),
            P(),
        ),
        check_vma=False,
    )
```

```python
import math

import jax
import jax.numpy as jnp
from jax import lax
from jax.sharding import PartitionSpec as P

HEADS = 12
BLK = 128
REACH = 16


exponent_divisor = 10.0
norm_eps = 1e-06


def padded(value, sides, width):
    for axis, dim in sides:
        size, length = (lax.axis_size(axis), value.shape[dim])
        up = [(i, (i + 1) % size) for i in range(size)]
        down = [(j, i) for i, j in up]
        last = lax.slice_in_dim(value, length - width, length, axis=dim)
        first = lax.slice_in_dim(value, 0, width, axis=dim)
        before = lax.ppermute(last, axis, up)
        after = lax.ppermute(first, axis, down)
        value = jnp.concatenate([before, value, after], axis=dim)
    return value


def passed_along(value, axis, steps):
    count = lax.axis_size(axis)
    pairs = [(source, (source + steps) % count) for source in range(count)]
    return lax.ppermute(value, axis, pairs)


def normalize(projected, head_dim):
    by_head = projected.reshape(projected.shape[:-1] + (projected.shape[-1] // head_dim, head_dim))
    length = jnp.sqrt(jnp.sum(by_head * by_head, -1, keepdims=True))
    divisor = jnp.maximum(length, 0.7 * math.sqrt(head_dim))
    return (by_head / divisor, divisor, length > 0.7 * math.sqrt(head_dim))


def unit_heads(projected, head_dim):
    unit, divisor, active = normalize(projected, head_dim)
    return unit.reshape(projected.shape)


def norm_back(projected, grad, head_dim):
    unit, divisor, active = normalize(projected, head_dim)
    along = grad.astype(jnp.float32).reshape(unit.shape)
    inner = jnp.sum(unit * along, -1, keepdims=True)
    result = (along - jnp.where(active, unit * inner, 0.0)) / divisor
    return result.reshape(projected.shape)


def xor_steps(axes):
    steps = []
    for axis in axes:
        size = lax.axis_size(axis)
        assert size & (size - 1) == 0
        mask = 1
        while mask < size:
            steps.append((axis, mask))
            mask *= 2
    return steps


def xor_swap(value, axis, mask):
    size = lax.axis_size(axis)
    return lax.ppermute(value, axis, [(i, i ^ mask) for i in range(size)])


def ordered_pair(held, received, bit):
    pair = jnp.stack([held, received])
    first = lax.dynamic_index_in_dim(pair, bit, 0, keepdims=False)
    second = lax.dynamic_index_in_dim(pair, 1 - bit, 0, keepdims=False)
    return jnp.concatenate([first, second], 0)


def butterfly_gather(value, axis):
    size = lax.axis_size(axis)
    held = value
    mask = 1
    while mask < size:
        bit = (lax.axis_index(axis) // mask) % 2
        held = ordered_pair(held, xor_swap(held, axis, mask), bit)
        mask *= 2
    return held


def scatter_steps(held, steps, wire):
    bits = []
    for axis, mask in steps:
        bit = (lax.axis_index(axis) // mask) % 2
        halves = held.reshape((2, held.shape[0] // 2) + held.shape[1:])
        keep = lax.dynamic_index_in_dim(halves, bit, 0, keepdims=False)
        send = lax.dynamic_index_in_dim(halves, 1 - bit, 0, keepdims=False)
        held = keep + xor_swap(send.astype(wire), axis, mask).astype(held.dtype)
        bits.append(bit)
    return held, bits


def gather_steps(held, steps, bits):
    for (axis, mask), bit in reversed(list(zip(steps, bits))):
        held = ordered_pair(held, xor_swap(held, axis, mask), bit)
    return held


def pad_rows(value, multiple):
    return jnp.concatenate(
        [value, jnp.zeros((-value.shape[0] % multiple,) + value.shape[1:], value.dtype)], 0
    )


def to_heads(value, blocks, heads_here, head_dim):
    lead = value.shape[:-2]
    value = value.reshape(lead + (blocks, BLK, heads_here, head_dim))
    return jnp.moveaxis(value, len(lead) + 2, len(lead))


def from_heads(value):
    lead = value.shape[:-4]
    heads_here, blocks, rows, head_dim = value.shape[len(lead) :]
    value = jnp.moveaxis(value, len(lead), len(lead) + 2)
    return value.reshape(lead + (blocks * rows, heads_here * head_dim))


def local(tokens, norm_gain, w_qkv, w_out, cotangent, neighbours, counts):
    f32, bf16 = jnp.float32, jnp.bfloat16
    width = tokens.shape[1]
    head_dim = width // HEADS
    n_head = lax.axis_size("head")
    n_slab = lax.axis_size("slab")
    head_cols = width // n_head
    heads_here = HEADS // n_head
    head_index = lax.axis_index("head")
    slab_index = lax.axis_index("slab")
    slab_blocks, n_slots = neighbours.shape
    ext_blocks = slab_blocks + 2 * REACH
    n_blocks = slab_blocks * n_slab
    tok_f32 = tokens.astype(f32)
    inverse = lax.rsqrt(jnp.mean(tok_f32 * tok_f32, -1, keepdims=True) + norm_eps)
    normed = (tok_f32 * inverse * norm_gain).astype(bf16)
    w_here = lax.dynamic_slice_in_dim(w_qkv, head_index * head_cols, head_cols, 2)
    slab_tok = butterfly_gather(tokens, "head").astype(f32)
    slab_inverse = lax.rsqrt(jnp.mean(slab_tok * slab_tok, -1, keepdims=True) + norm_eps)
    slab_scaled = slab_tok * slab_inverse
    gathered = (slab_scaled * norm_gain).astype(bf16)
    projected = jnp.einsum("rd,cde->cre", gathered, w_here, preferred_element_type=f32)
    packed = jnp.stack(
        [unit_heads(projected[0], head_dim), unit_heads(projected[1], head_dim), projected[2]]
    ).astype(bf16)
    split = lambda value: to_heads(value, slab_blocks, heads_here, head_dim)
    q_heads = split(packed[0])
    lookup = (neighbours - slab_index * slab_blocks + REACH) % n_blocks
    choose = lookup[:, :, None] == jnp.arange(ext_blocks, dtype=jnp.int32)
    fetch = lambda value: jnp.einsum(
        "bse,hekd->hbskd",
        choose.astype(bf16),
        padded(split(value), (("slab", 1),), REACH),
        preferred_element_type=f32,
    ).astype(bf16)
    keys, values = fetch(packed[1]), fetch(packed[2])
    live = (jnp.arange(n_slots, dtype=jnp.int32)[None, :] < counts[:, None]).astype(f32)
    scores = exponent_divisor * jnp.einsum(
        "hbqd,hbskd->hbqsk", q_heads, keys, preferred_element_type=f32
    )
    raised = jnp.exp(scores) * live[None, :, None, :, None]
    weights = raised / jnp.sum(raised, (-2, -1), keepdims=True)
    weights_bf = weights.astype(bf16)
    attended_heads = jnp.einsum(
        "hbqsk,hbskd->hbqd", weights_bf, values, preferred_element_type=f32
    ).astype(bf16)
    attended = lax.all_to_all(
        from_heads(attended_heads), "head", split_axis=0, concat_axis=1, tiled=True
    )
    output = (tok_f32 + jnp.dot(attended, w_out, preferred_element_type=f32)).astype(bf16)
    d_out_part = jnp.dot(attended.T, cotangent, preferred_element_type=f32)
    d_attended = jnp.dot(cotangent, w_out.T, preferred_element_type=f32).astype(bf16)
    d_attended, keys = lax.optimization_barrier((d_attended, keys))
    d_attn = split(lax.all_to_all(d_attended, "head", split_axis=1, concat_axis=0, tiled=True))
    d_weights = jnp.einsum("hbqd,hbskd->hbqsk", d_attn, values, preferred_element_type=f32)
    row_dot = jnp.sum(d_weights * weights, (-2, -1), keepdims=True)
    d_scores = (exponent_divisor * weights * (d_weights - row_dot)).astype(bf16)
    attended, d_scores = lax.optimization_barrier((attended, d_scores))
    d_query = jnp.einsum("hbqsk,hbskd->hbqd", d_scores, keys, preferred_element_type=f32)
    d_keys = jnp.einsum("hbqsk,hbqd->hbskd", d_scores, q_heads, preferred_element_type=f32)
    d_values = jnp.einsum("hbqsk,hbqd->hbskd", weights_bf, d_attn, preferred_element_type=f32)
    scatter = lambda grads: jnp.einsum(
        "bse,hbskd->hekd",
        choose.astype(f32),
        grads,
        precision=lax.Precision.DEFAULT,
        preferred_element_type=f32,
    )
    grad_ext = jnp.stack([scatter(d_keys), scatter(d_values)])
    low_rim = grad_ext[:, :, :REACH]
    high_rim = grad_ext[:, :, REACH + slab_blocks :]
    from_above = passed_along(low_rim.astype(bf16), "slab", -1).astype(f32)
    from_below = passed_along(high_rim.astype(bf16), "slab", 1).astype(f32)
    own_grads = grad_ext[:, :, REACH : REACH + slab_blocks]
    own_grads = own_grads.at[:, :, slab_blocks - REACH :].add(from_above)
    own_grads = own_grads.at[:, :, :REACH].add(from_below)
    d_packed = jnp.concatenate(
        [from_heads(d_query)[None], from_heads(own_grads)], 0
    ).astype(bf16)
    d_query_part = norm_back(projected[0], d_packed[0], head_dim).astype(bf16)
    d_key_part = norm_back(projected[1], d_packed[1], head_dim).astype(bf16)
    d_qkv = jnp.stack([d_query_part, d_key_part, d_packed[2]])
    d_normed_part = jnp.einsum("crk,cdk->rd", d_qkv, w_here, preferred_element_type=f32)
    d_gain_part = jnp.sum(d_normed_part * slab_scaled, 0)
    shares = d_normed_part.astype(bf16).reshape(n_head, -1, width)
    d_qkv_part = jnp.einsum("rd,crk->cdk", gathered, d_qkv, preferred_element_type=f32)
    head_steps, slab_steps = xor_steps(("head",)), xor_steps(("slab",))
    sub = 8
    wide = pad_rows(jnp.concatenate([d_out_part, d_gain_part[None]], 0), n_head * sub)
    wide_part, head_bits = scatter_steps(wide, head_steps, bf16)
    wide_part, shares = lax.optimization_barrier((wide_part, shares))
    received = lax.all_to_all(shares, "head", split_axis=0, concat_axis=0, tiled=True)
    narrow = d_qkv_part.reshape(-1, width)
    both = pad_rows(jnp.concatenate([narrow, wide_part], 0), n_slab)
    both_part, slab_bits = scatter_steps(both, slab_steps, bf16)
    both = gather_steps(both_part.astype(bf16), slab_steps, slab_bits)
    narrow_rows = narrow.shape[0]
    wide_part = both[narrow_rows : narrow_rows + wide_part.shape[0]]
    wide_part, received = lax.optimization_barrier((wide_part, received))
    wide = gather_steps(wide_part, head_steps, head_bits).astype(f32)
    d_w_qkv = both[:narrow_rows].astype(f32).reshape(d_qkv_part.shape)
    d_w_out = wide[:width]
    d_gain = wide[width]
    d_normed = jnp.sum(received.astype(f32), 0)
    scaled = d_normed * norm_gain
    d_tokens = (
        cotangent.astype(f32)
        + inverse * scaled
        - tok_f32 * inverse**3 * jnp.mean(scaled * tok_f32, -1, keepdims=True)
    )
    return (output, d_tokens.astype(bf16), d_w_qkv, d_w_out, d_gain)


def solution(mesh):
    placed = (
        P(("slab", "head"), None),
        P(),
        P(),
        P(),
        P(("slab", "head"), None),
        P("slab", None),
        P("slab"),
    )
    return jax.shard_map(
        local,
        mesh=mesh,
        in_specs=placed,
        out_specs=(
            P(("slab", "head"), None),
            P(("slab", "head"), None),
            P(None, None, "head"),
            P(),
            P(),
        ),
        check_vma=False,
    )
```

```python
import math

import jax
import jax.numpy as jnp
from jax import lax
from jax.sharding import PartitionSpec as P

HEADS = 12
BLK = 128
REACH = 16


exponent_divisor = 10.0
norm_eps = 1e-06


def padded(value, sides, width):
    for axis, dim in sides:
        size, length = (lax.axis_size(axis), value.shape[dim])
        up = [(i, (i + 1) % size) for i in range(size)]
        down = [(j, i) for i, j in up]
        last = lax.slice_in_dim(value, length - width, length, axis=dim)
        first = lax.slice_in_dim(value, 0, width, axis=dim)
        before = lax.ppermute(last, axis, up)
        after = lax.ppermute(first, axis, down)
        value = jnp.concatenate([before, value, after], axis=dim)
    return value


def passed_along(value, axis, steps):
    count = lax.axis_size(axis)
    pairs = [(source, (source + steps) % count) for source in range(count)]
    return lax.ppermute(value, axis, pairs)


def normalize(projected, head_dim):
    by_head = projected.reshape(projected.shape[:-1] + (projected.shape[-1] // head_dim, head_dim))
    length = jnp.sqrt(jnp.sum(by_head * by_head, -1, keepdims=True))
    divisor = jnp.maximum(length, 0.7 * math.sqrt(head_dim))
    return (by_head / divisor, divisor, length > 0.7 * math.sqrt(head_dim))


def unit_heads(projected, head_dim):
    unit, divisor, active = normalize(projected, head_dim)
    return unit.reshape(projected.shape)


def norm_back(projected, grad, head_dim):
    unit, divisor, active = normalize(projected, head_dim)
    along = grad.astype(jnp.float32).reshape(unit.shape)
    inner = jnp.sum(unit * along, -1, keepdims=True)
    result = (along - jnp.where(active, unit * inner, 0.0)) / divisor
    return result.reshape(projected.shape)


def xor_steps(axes):
    steps = []
    for axis in axes:
        size = lax.axis_size(axis)
        assert size & (size - 1) == 0
        mask = 1
        while mask < size:
            steps.append((axis, mask))
            mask *= 2
    return steps


def xor_swap(value, axis, mask):
    size = lax.axis_size(axis)
    return lax.ppermute(value, axis, [(i, i ^ mask) for i in range(size)])


def ordered_pair(held, received, bit):
    pair = jnp.stack([held, received])
    first = lax.dynamic_index_in_dim(pair, bit, 0, keepdims=False)
    second = lax.dynamic_index_in_dim(pair, 1 - bit, 0, keepdims=False)
    return jnp.concatenate([first, second], 0)


def butterfly_gather(value, axis):
    size = lax.axis_size(axis)
    held = value
    mask = 1
    while mask < size:
        bit = (lax.axis_index(axis) // mask) % 2
        held = ordered_pair(held, xor_swap(held, axis, mask), bit)
        mask *= 2
    return held


def scatter_steps(held, steps, wire):
    bits = []
    for axis, mask in steps:
        bit = (lax.axis_index(axis) // mask) % 2
        halves = held.reshape((2, held.shape[0] // 2) + held.shape[1:])
        keep = lax.dynamic_index_in_dim(halves, bit, 0, keepdims=False)
        send = lax.dynamic_index_in_dim(halves, 1 - bit, 0, keepdims=False)
        held = keep + xor_swap(send.astype(wire), axis, mask).astype(held.dtype)
        bits.append(bit)
    return held, bits


def gather_steps(held, steps, bits):
    for (axis, mask), bit in reversed(list(zip(steps, bits))):
        held = ordered_pair(held, xor_swap(held, axis, mask), bit)
    return held


def pad_rows(value, multiple):
    return jnp.concatenate(
        [value, jnp.zeros((-value.shape[0] % multiple,) + value.shape[1:], value.dtype)], 0
    )


def to_heads(value, blocks, heads_here, head_dim):
    lead = value.shape[:-2]
    value = value.reshape(lead + (blocks, BLK, heads_here, head_dim))
    return jnp.moveaxis(value, len(lead) + 2, len(lead))


def from_heads(value):
    lead = value.shape[:-4]
    heads_here, blocks, rows, head_dim = value.shape[len(lead) :]
    value = jnp.moveaxis(value, len(lead), len(lead) + 2)
    return value.reshape(lead + (blocks * rows, heads_here * head_dim))


def local(tokens, norm_gain, w_qkv, w_out, cotangent, neighbours, counts):
    f32, bf16 = jnp.float32, jnp.bfloat16
    width = tokens.shape[1]
    head_dim = width // HEADS
    n_head = lax.axis_size("head")
    n_slab = lax.axis_size("slab")
    head_cols = width // n_head
    heads_here = HEADS // n_head
    head_index = lax.axis_index("head")
    slab_index = lax.axis_index("slab")
    slab_blocks, n_slots = neighbours.shape
    ext_blocks = slab_blocks + 2 * REACH
    n_blocks = slab_blocks * n_slab
    tok_f32 = tokens.astype(f32)
    inverse = lax.rsqrt(jnp.mean(tok_f32 * tok_f32, -1, keepdims=True) + norm_eps)
    normed = (tok_f32 * inverse * norm_gain).astype(bf16)
    w_here = lax.dynamic_slice_in_dim(w_qkv, head_index * head_cols, head_cols, 2)
    slab_tok = butterfly_gather(tokens, "head").astype(f32)
    slab_inverse = lax.rsqrt(jnp.mean(slab_tok * slab_tok, -1, keepdims=True) + norm_eps)
    slab_scaled = slab_tok * slab_inverse
    gathered = (slab_scaled * norm_gain).astype(bf16)
    projected = jnp.einsum("rd,cde->cre", gathered, w_here, preferred_element_type=f32)
    packed = jnp.stack(
        [unit_heads(projected[0], head_dim), unit_heads(projected[1], head_dim), projected[2]]
    ).astype(bf16)
    split = lambda value: to_heads(value, slab_blocks, heads_here, head_dim)
    q_heads = split(packed[0])
    lookup = (neighbours - slab_index * slab_blocks + REACH) % n_blocks
    choose = lookup[:, :, None] == jnp.arange(ext_blocks, dtype=jnp.int32)
    fetch = lambda value: jnp.einsum(
        "bse,hekd->hbskd",
        choose.astype(bf16),
        padded(split(value), (("slab", 1),), REACH),
        preferred_element_type=f32,
    ).astype(bf16)
    keys, values = fetch(packed[1]), fetch(packed[2])
    live = (jnp.arange(n_slots, dtype=jnp.int32)[None, :] < counts[:, None]).astype(f32)
    scores = exponent_divisor * jnp.einsum(
        "hbqd,hbskd->hbqsk", q_heads, keys, preferred_element_type=f32
    )
    raised = jnp.exp(scores) * live[None, :, None, :, None]
    weights = raised * (1.0 / jnp.sum(raised, (-2, -1), keepdims=True))
    weights_bf = weights.astype(bf16)
    attended_heads = jnp.einsum(
        "hbqsk,hbskd->hbqd", weights_bf, values, preferred_element_type=f32
    ).astype(bf16)
    attended = lax.all_to_all(
        from_heads(attended_heads), "head", split_axis=0, concat_axis=1, tiled=True
    )
    output = (tok_f32 + jnp.dot(attended, w_out, preferred_element_type=f32)).astype(bf16)
    d_out_part = jnp.dot(attended.T, cotangent, preferred_element_type=f32)
    d_attended = jnp.dot(cotangent, w_out.T, preferred_element_type=f32).astype(bf16)
    d_attended, keys = lax.optimization_barrier((d_attended, keys))
    d_attn = split(lax.all_to_all(d_attended, "head", split_axis=1, concat_axis=0, tiled=True))
    d_weights = jnp.einsum("hbqd,hbskd->hbqsk", d_attn, values, preferred_element_type=f32)
    row_dot = jnp.sum(d_weights * weights, (-2, -1), keepdims=True)
    d_scores = (exponent_divisor * weights * (d_weights - row_dot)).astype(bf16)
    attended, d_scores = lax.optimization_barrier((attended, d_scores))
    d_query = jnp.einsum("hbqsk,hbskd->hbqd", d_scores, keys, preferred_element_type=f32)
    d_keys = jnp.einsum("hbqsk,hbqd->hbskd", d_scores, q_heads, preferred_element_type=f32)
    d_values = jnp.einsum("hbqsk,hbqd->hbskd", weights_bf, d_attn, preferred_element_type=f32)
    scatter = lambda grads: jnp.einsum(
        "bse,hbskd->hekd",
        choose.astype(f32),
        grads,
        precision=lax.Precision.DEFAULT,
        preferred_element_type=f32,
    )
    grad_ext = jnp.stack([scatter(d_keys), scatter(d_values)])
    low_rim = grad_ext[:, :, :REACH]
    high_rim = grad_ext[:, :, REACH + slab_blocks :]
    from_above = passed_along(low_rim.astype(bf16), "slab", -1).astype(f32)
    from_below = passed_along(high_rim.astype(bf16), "slab", 1).astype(f32)
    own_grads = grad_ext[:, :, REACH : REACH + slab_blocks]
    own_grads = own_grads.at[:, :, slab_blocks - REACH :].add(from_above)
    own_grads = own_grads.at[:, :, :REACH].add(from_below)
    d_packed = jnp.concatenate(
        [from_heads(d_query)[None], from_heads(own_grads)], 0
    ).astype(bf16)
    d_query_part = norm_back(projected[0], d_packed[0], head_dim).astype(bf16)
    d_key_part = norm_back(projected[1], d_packed[1], head_dim).astype(bf16)
    d_qkv = jnp.stack([d_query_part, d_key_part, d_packed[2]])
    d_normed_part = jnp.einsum("crk,cdk->rd", d_qkv, w_here, preferred_element_type=f32)
    d_gain_part = jnp.sum(d_normed_part * slab_scaled, 0)
    shares = d_normed_part.astype(bf16).reshape(n_head, -1, width)
    d_qkv_part = jnp.einsum("rd,crk->cdk", gathered, d_qkv, preferred_element_type=f32)
    head_steps, slab_steps = xor_steps(("head",)), xor_steps(("slab",))
    sub = 8
    wide = pad_rows(jnp.concatenate([d_out_part, d_gain_part[None]], 0), n_head * sub)
    wide_part, head_bits = scatter_steps(wide, head_steps, bf16)
    wide_part, shares = lax.optimization_barrier((wide_part, shares))
    received = lax.all_to_all(shares, "head", split_axis=0, concat_axis=0, tiled=True)
    narrow = d_qkv_part.reshape(-1, width)
    both = pad_rows(jnp.concatenate([narrow, wide_part], 0), n_slab)
    both_part, slab_bits = scatter_steps(both, slab_steps, bf16)
    both = gather_steps(both_part.astype(bf16), slab_steps, slab_bits)
    narrow_rows = narrow.shape[0]
    wide_part = both[narrow_rows : narrow_rows + wide_part.shape[0]]
    wide_part, received = lax.optimization_barrier((wide_part, received))
    wide = gather_steps(wide_part, head_steps, head_bits).astype(f32)
    d_w_qkv = both[:narrow_rows].astype(f32).reshape(d_qkv_part.shape)
    d_w_out = wide[:width]
    d_gain = wide[width]
    d_normed = jnp.sum(received.astype(f32), 0)
    scaled = d_normed * norm_gain
    d_tokens = (
        cotangent.astype(f32)
        + inverse * scaled
        - tok_f32 * inverse**3 * jnp.mean(scaled * tok_f32, -1, keepdims=True)
    )
    return (output, d_tokens.astype(bf16), d_w_qkv, d_w_out, d_gain)


def solution(mesh):
    placed = (
        P(("slab", "head"), None),
        P(),
        P(),
        P(),
        P(("slab", "head"), None),
        P("slab", None),
        P("slab"),
    )
    return jax.shard_map(
        local,
        mesh=mesh,
        in_specs=placed,
        out_specs=(
            P(("slab", "head"), None),
            P(("slab", "head"), None),
            P(None, None, "head"),
            P(),
            P(),
        ),
        check_vma=False,
    )
```
